32 devices in a mesh: gx: 8 (over y, x, core), gy: 4 (over z).
Axes of the slice: x: 2, y: 2, z: 4, core: 2. Of those that a mesh axis runs over, the one named last changes fastest.
Arguments:
- coords: float32 [8, 65536], P(None, ('gx', 'gy')), may hold values from -6 to 6
- inv_scale: float32 [8], replicated, may hold values from 0.3 to 0.8
- noise: float32 [65536], P(('gx', 'gy')), may hold values from 0.3 to 1
- right_side: float32 [16, 65536], P(None, ('gx', 'gy')), may hold values from -20 to 20
- basis: float32 [128, 65536], P(None, ('gx', 'gy')), may hold values from -0.125 to 0.125
- level_gain: float32 [5, 65536], P(None, ('gx', 'gy')), may hold values from 0.5 to 2
- coupling: float32 [5, 128, 128], replicated, may hold values from -0.5 to 0.5
- order: int32 [32, 2048], P(('gx', 'gy')), may hold values from 0 to 2047, each once within a row
- pairs: int32 [32, 2, 4], P(('gx', 'gy')), may hold values from 0 to 7
Outputs:
- solution: float32 [16, 65536], P(None, ('gx', 'gy'))
- residual: float32 [16, 65536], P(None, ('gx', 'gy'))
The draws below stay inside these ranges and needn't reach their ends.
Inputs may be any that keep to these rules, and one draw needn't show every extreme that they name: Each row of order is a permutation of 0 .. 2047. `pairs`: every entry names a tile of its own leaf.
All inputs are finite; a program needn't handle non-finite values.
Results may differ from the reference program's by a relative error of at most 0.0003.
Values sent between devices are 32-bit elements; how exact they have to be, the bound alone decides.
No kernel may reach another device: no remote copies, remote signals or barrier semaphores. Data moves between devices by JAX's collectives and lax.ppermute only.
A program may use at most 64 MiB of HBM per device.

```python
import math
import jax
import jax.numpy as jnp
from jax import lax

FEATURES = 8
LOW_RANK = 128
COLUMNS = 16
TILE_POINTS = 256
ITERATIONS = 2
LEAF_POINTS = 2048
TILE_PAIRS = 4
LEAF_TILES = 8
LEAVES = 32
POINTS = 65536
LEVELS = 5


def draw_right_side(key, part):
    position = jnp.arange(POINTS, dtype=jnp.float32) / POINTS
    base = jax.random.truncated_normal(key, -6.0, 6.0, (COLUMNS, POINTS), jnp.float32)
    return base * (1.0 + 2.0 * position)[None, :]


def set_ends(drawn, stream_key, least, high):
    dims = drawn.shape
    index_at = [jax.random.randint(jax.random.fold_in(stream_key, axis), (), 0, dims[axis]) for axis in range(len(dims))]
    drawn = drawn.at[tuple(index_at)].set(least)
    longest = dims.index(max(dims))
    index_at[longest] = (index_at[longest] + 1) % dims[longest]
    return drawn.at[tuple(index_at)].set(high)


def block_scale(key, shape, pieces, smallest, largest):
    factor_of = 1.0
    for axis_at, blocks in pieces:
        steps = jax.random.uniform(jax.random.fold_in(jax.random.fold_in(key, 6), axis_at), (blocks,), jnp.float32, smallest / len(pieces), largest / len(pieces))
        factor_of = factor_of * jnp.repeat(jnp.exp(steps), shape[axis_at] // blocks).reshape((-1,) + (1,) * (len(shape) - 1 - axis_at))
    return factor_of


def bell_draw(key, shape, spread, limit, pieces=(), kind=jnp.bfloat16):
    drawn = jax.random.normal(key, shape, jnp.float32) * spread
    if len(pieces) > 0:
        drawn = block_scale(key, shape, pieces, -0.22, 0.18) * drawn
    return jnp.clip(drawn, min=-limit, max=limit).astype(kind)


def setup_inputs(seed: int = 0) -> dict:
    keys = jax.random.split(jax.random.key(seed), 10)
    coords = bell_draw(keys[0], (FEATURES, POINTS), 1.0, 6.0, ((1, 32),), jnp.float32)
    inv_scale = jnp.clip(jnp.exp(jax.random.uniform(keys[1], (FEATURES,), jnp.float32, math.log(0.3), math.log(0.8))), 0.3, 0.8)
    noise = jnp.clip(jnp.exp(math.log(1.0) - 1.2039728 * jax.random.uniform(keys[2], (POINTS,), jnp.float32) ** block_scale(keys[2], (POINTS,), ((0, 32),), -0.2, 0.2)), 0.3, 1.0)
    right_side = draw_right_side(jax.random.fold_in(keys[9], 71), 0)
    basis = bell_draw(keys[4], (LOW_RANK, POINTS), LEAF_POINTS ** -0.5, 0.125, ((1, 32),), jnp.float32)
    level_gain = jnp.clip(jnp.exp(math.log(2.0) - 1.3862944 * jax.random.uniform(keys[5], (LEVELS, POINTS), jnp.float32) ** block_scale(keys[5], (LEVELS, POINTS), ((1, 32),), -0.2, 0.2)), 0.5, 2.0)
    coupling = bell_draw(keys[6], (LEVELS, LOW_RANK, LOW_RANK), LOW_RANK ** -0.5, 0.5, (), jnp.float32)
    order = jax.vmap(lambda own: jax.random.permutation(own, LEAF_POINTS))(jax.random.split(keys[7], LEAVES)).reshape((LEAVES, LEAF_POINTS)).astype(jnp.int32)
    pairs = set_ends(jax.random.randint(keys[8], (LEAVES, 2, TILE_PAIRS), 0, LEAF_TILES), jax.random.fold_in(keys[8], 1), 0, LEAF_TILES - 1).astype(jnp.int32)
    return dict(coords=coords, inv_scale=inv_scale, noise=noise, right_side=right_side, basis=basis, level_gain=level_gain, coupling=coupling, order=order, pairs=pairs)


near_weight = 0.25
highest = lax.Precision.HIGHEST


def tile_near(tile_coords, tile_vec, pair_rows, pair_cols):
    width = tile_coords.shape[2]
    union = jnp.concatenate([tile_coords[:, pair_rows], tile_coords[:, pair_cols]], axis=2)
    gram = jnp.einsum('fgi,fgj->gij', union, union, precision=highest)
    square = jnp.sum(union * union, axis=0)
    dist = square[:, :, None] + square[:, None, :] - 2.0 * gram
    kern = near_weight * jnp.exp(-0.5 * dist)
    union_vec = jnp.concatenate([tile_vec[:, pair_rows], tile_vec[:, pair_cols]], axis=2)
    result = jnp.einsum('gij,cgj->cgi', kern, union_vec, precision=highest)
    tile_ids = jnp.arange(tile_coords.shape[1], dtype=jnp.int32)
    row_hot = (pair_rows[:, None] == tile_ids[None, :]).astype(tile_vec.dtype)
    col_hot = (pair_cols[:, None] == tile_ids[None, :]).astype(tile_vec.dtype)
    added = jnp.einsum('cgi,gt->cti', result[:, :, :width], row_hot, precision=highest)
    return added + jnp.einsum('cgi,gt->cti', result[:, :, width:], col_hot, precision=highest)


def near_field(tile_coords, tile_vec, pair_rows, pair_cols):
    group = math.gcd(pair_rows.shape[0], 4)
    rows = pair_rows.reshape(-1, group)
    cols = pair_cols.reshape(-1, group)

    def accumulate(total, picked):
        return total + tile_near(tile_coords, tile_vec, picked[0], picked[1]), None

    total, unused = lax.scan(accumulate, jnp.zeros(tile_vec.shape, tile_vec.dtype), (rows, cols))
    return total


def apply_kernel(vector, coords, inv_scale, noise, basis, level_gain, coupling, order, pairs):
    leaf_vec = vector.reshape(COLUMNS, LEAVES, LEAF_POINTS).transpose(1, 0, 2)
    leaf_gain = level_gain.reshape(LEVELS, LEAVES, LEAF_POINTS).transpose(1, 0, 2)
    leaf_basis = basis.reshape(LOW_RANK, LEAVES, LEAF_POINTS).transpose(1, 0, 2)
    leaf_coords = (coords * inv_scale[:, None]).reshape(FEATURES, LEAVES, LEAF_POINTS).transpose(1, 0, 2)
    leaf_noise = noise.reshape(LEAVES, LEAF_POINTS)

    def project(items):
        gains, values, bases = items
        return jnp.einsum('lp,cp,rp->lcr', gains, values, bases, precision=highest)

    proj = lax.map(project, (leaf_gain, leaf_vec, leaf_basis))
    sums = []
    for level in range(LEVELS):
        group = 2 ** (level + 1)
        block = proj[:, level].reshape(LEAVES // group, group, COLUMNS, LOW_RANK).sum(axis=1)
        sums.append(jnp.repeat(block, group, axis=0))
    nodesum = jnp.stack(sums, axis=1)
    scales = 2.0 ** ((1.0 - jnp.arange(LEVELS, dtype=jnp.float32)) / 2.0)
    coupled = jnp.einsum('qlcr,lrs->qlcs', nodesum, coupling, precision=highest)
    coupled = jnp.einsum('qlcs,lrs->qlcr', coupled, coupling, precision=highest) * scales[None, :, None, None]

    def leaf_apply(items):
        values, gains, bases, points, noises, couples, perm, listed = items
        back = jnp.einsum('lcr,rp->lcp', couples, bases, precision=highest)
        far = jnp.sum(back * gains[:, None, :], axis=0)
        tile_coords = points[:, perm].reshape(FEATURES, LEAF_TILES, TILE_POINTS)
        tile_vec = values[:, perm].reshape(COLUMNS, LEAF_TILES, TILE_POINTS)
        near_t = near_field(tile_coords, tile_vec, listed[0], listed[1]).reshape(COLUMNS, LEAF_POINTS)
        near = jnp.zeros_like(values).at[:, perm].set(near_t)
        return noises[None, :] * values + far + near

    result = lax.map(leaf_apply, (leaf_vec, leaf_gain, leaf_basis, leaf_coords, leaf_noise, coupled, order, pairs))
    return result.transpose(1, 0, 2).reshape(COLUMNS, POINTS)


def reference(coords, inv_scale, noise, right_side, basis, level_gain, coupling, order, pairs):
    solution = jnp.zeros_like(right_side)
    residual = right_side
    direction = right_side
    norm_now = jnp.sum(residual * residual, axis=1)
    for step in range(ITERATIONS):
        image = apply_kernel(direction, coords, inv_scale, noise, basis, level_gain, coupling, order, pairs)
        alpha = norm_now / jnp.sum(direction * image, axis=1)
        solution = solution + alpha[:, None] * direction
        residual = residual - alpha[:, None] * image
        if step + 1 < ITERATIONS:
            norm_next = jnp.sum(residual * residual, axis=1)
            direction = residual + (norm_next / norm_now)[:, None] * direction
            norm_now = norm_next
    return solution, residual
```

```python
import math

import jax
import jax.numpy as jnp
from jax import lax
from jax.sharding import PartitionSpec as P

TILE_POINTS = 256
ITERATIONS = 2


near_weight = 0.25
highest = lax.Precision.HIGHEST


def swapped(value, axis, bit):
    mask = 2**bit
    pairs = [(source, source ^ mask) for source in range(lax.axis_size(axis))]
    return lax.ppermute(value, axis, pairs)


def tile_near(tile_coords, tile_vec, pair_rows, pair_cols):
    width = tile_coords.shape[2]
    union = jnp.concatenate([tile_coords[:, pair_rows], tile_coords[:, pair_cols]], axis=2)
    gram = jnp.einsum("fgi,fgj->gij", union, union, precision=highest)
    square = jnp.sum(union * union, axis=0)
    dist = square[:, :, None] + square[:, None, :] - 2.0 * gram
    kern = near_weight * jnp.exp(-0.5 * dist)
    union_vec = jnp.concatenate([tile_vec[:, pair_rows], tile_vec[:, pair_cols]], axis=2)
    result = jnp.einsum("gij,cgj->cgi", kern, union_vec, precision=highest)
    tile_ids = jnp.arange(tile_coords.shape[1], dtype=jnp.int32)
    row_hot = (pair_rows[:, None] == tile_ids[None, :]).astype(jnp.float32)
    col_hot = (pair_cols[:, None] == tile_ids[None, :]).astype(jnp.float32)
    added = jnp.einsum("cgi,gt->cti", result[:, :, :width], row_hot, precision=highest)
    return added + jnp.einsum("cgi,gt->cti", result[:, :, width:], col_hot, precision=highest)


def near_field(tile_coords, tile_vec, pair_rows, pair_cols):
    group = math.gcd(pair_rows.shape[0], 4)
    rows = pair_rows.reshape(-1, group)
    cols = pair_cols.reshape(-1, group)

    def accumulate(total, picked):
        return (total + tile_near(tile_coords, tile_vec, picked[0], picked[1]), None)

    total, unused = lax.scan(accumulate, jnp.zeros(tile_vec.shape, jnp.float32), (rows, cols))
    return total


def tree_sums(proj):
    low_count = lax.axis_size("gy").bit_length() - 1
    high_count = lax.axis_size("gx").bit_length() - 1
    running = proj
    for bit in range(low_count):
        partner = swapped(running[bit:], "gy", bit)
        running = jnp.concatenate([running[:bit], running[bit:] + partner], axis=0)
    for bit in range(high_count):
        level = low_count + bit
        partner = swapped(running[level:], "gx", bit)
        running = jnp.concatenate([running[:level], running[level:] + partner], axis=0)
    return running


def butterfly(value):
    for bit in range(lax.axis_size("gy").bit_length() - 1):
        value = value + swapped(value, "gy", bit)
    for bit in range(lax.axis_size("gx").bit_length() - 1):
        value = value + swapped(value, "gx", bit)
    return value


def per_device(coords, inv_scale, noise, right_side, basis, level_gain, coupling, order, pairs):
    perm = order[0]
    points = right_side.shape[1]
    columns = right_side.shape[0]
    tiles = points // TILE_POINTS
    levels = level_gain.shape[0]
    rank = basis.shape[0]
    tile_coords = (coords * inv_scale[:, None])[:, perm].reshape(
        coords.shape[0], tiles, TILE_POINTS
    )
    noise_t = noise[perm]
    gain_t = level_gain[:, perm]
    basis_t = basis[:, perm]
    rhs_t = right_side[:, perm]
    pair_rows = pairs[0, 0]
    pair_cols = pairs[0, 1]
    scales = 2.0 ** ((1.0 - jnp.arange(levels, dtype=jnp.float32)) / 2.0)
    solution = jnp.zeros_like(rhs_t)
    residual = rhs_t
    direction = rhs_t

    def sums_with_norm(values):
        proj = jnp.einsum("lp,cp,rp->lcr", gain_t, values, basis_t, precision=highest)
        norm = jnp.sum(values * values, axis=1)
        extra = jnp.broadcast_to(norm[None, :, None], (1, columns, rank))
        running = tree_sums(jnp.concatenate([proj, extra], axis=0))
        return running[:levels], running[levels, :, 0]

    nodesum = None
    norm_now = None
    for step in range(ITERATIONS):
        if step == 0:
            nodesum, norm_now = sums_with_norm(residual)
        else:
            residual_sum, norm_next = sums_with_norm(residual)
            ratio = norm_next / norm_now
            direction = residual + ratio[:, None] * direction
            nodesum = residual_sum + ratio[None, :, None] * nodesum
            norm_now = norm_next
        coupled = jnp.einsum("lcr,lrs->lcs", nodesum, coupling, precision=highest)
        coupled = (
            jnp.einsum("lcs,lrs->lcr", coupled, coupling, precision=highest) * scales[:, None, None]
        )
        back = jnp.einsum("lcr,rp->lcp", coupled, basis_t, precision=highest)
        far = jnp.sum(back * gain_t[:, None, :], axis=0)
        near = near_field(
            tile_coords, direction.reshape(columns, tiles, TILE_POINTS), pair_rows, pair_cols
        )
        image = noise_t[None, :] * direction + far + near.reshape(columns, points)
        curve = butterfly(jnp.sum(direction * image, axis=1))
        alpha = norm_now / curve
        solution = solution + alpha[:, None] * direction
        residual = residual - alpha[:, None] * image
    inverse = jnp.zeros_like(perm).at[perm].set(jnp.arange(points, dtype=jnp.int32))
    return (solution[:, inverse], residual[:, inverse])


def solution(mesh):
    return jax.shard_map(
        per_device,
        mesh=mesh,
        in_specs=(
            P(None, ("gx", "gy")),
            P(),
            P(("gx", "gy")),
            P(None, ("gx", "gy")),
            P(None, ("gx", "gy")),
            P(None, ("gx", "gy")),
            P(),
            P(("gx", "gy"), None),
            P(("gx", "gy"), None, None),
        ),
        out_specs=(P(None, ("gx", "gy")), P(None, ("gx", "gy"))),
        check_vma=False,
    )
```

```python
import math

import jax
import jax.numpy as jnp
from jax import lax
from jax.sharding import PartitionSpec as P

TILE_POINTS = 256
ITERATIONS = 2


near_weight = 0.25
highest = lax.Precision.HIGHEST


def swapped(value, axis, bit):
    mask = 2**bit
    pairs = [(source, source ^ mask) for source in range(lax.axis_size(axis))]
    return lax.ppermute(value, axis, pairs)


def near_kernels(tile_coords, pair_rows, pair_cols):
    union = jnp.concatenate([tile_coords[:, pair_rows], tile_coords[:, pair_cols]], axis=2)
    gram = jnp.einsum("fgi,fgj->gij", union, union, precision=highest)
    square = jnp.sum(union * union, axis=0)
    dist = square[:, :, None] + square[:, None, :] - 2.0 * gram
    return near_weight * jnp.exp(-0.5 * dist)


def near_apply(kern, tile_vec, pair_rows, pair_cols):
    width = tile_vec.shape[2]
    union_vec = jnp.concatenate([tile_vec[:, pair_rows], tile_vec[:, pair_cols]], axis=2)
    result = jnp.einsum("gij,cgj->cgi", kern, union_vec, precision=highest)
    tile_ids = jnp.arange(tile_vec.shape[1], dtype=jnp.int32)
    row_hot = (pair_rows[:, None] == tile_ids[None, :]).astype(jnp.float32)
    col_hot = (pair_cols[:, None] == tile_ids[None, :]).astype(jnp.float32)
    added = jnp.einsum("cgi,gt->cti", result[:, :, :width], row_hot, precision=highest)
    return added + jnp.einsum("cgi,gt->cti", result[:, :, width:], col_hot, precision=highest)


def tree_sums(proj):
    low_count = lax.axis_size("gy").bit_length() - 1
    high_count = lax.axis_size("gx").bit_length() - 1
    running = proj
    for bit in range(low_count):
        partner = swapped(running[bit:], "gy", bit)
        running = jnp.concatenate([running[:bit], running[bit:] + partner], axis=0)
    for bit in range(high_count):
        level = low_count + bit
        partner = swapped(running[level:], "gx", bit)
        running = jnp.concatenate([running[:level], running[level:] + partner], axis=0)
    return running


def butterfly(value):
    for bit in range(lax.axis_size("gy").bit_length() - 1):
        value = value + swapped(value, "gy", bit)
    for bit in range(lax.axis_size("gx").bit_length() - 1):
        value = value + swapped(value, "gx", bit)
    return value


def per_device(coords, inv_scale, noise, right_side, basis, level_gain, coupling, order, pairs):
    perm = order[0]
    columns, points = right_side.shape
    tiles = points // TILE_POINTS
    levels = level_gain.shape[0]
    rank = basis.shape[0]
    pair_rows = pairs[0, 0]
    pair_cols = pairs[0, 1]
    inverse = jnp.zeros_like(perm).at[perm].set(jnp.arange(points, dtype=jnp.int32))
    tile_coords = (coords * inv_scale[:, None])[:, perm].reshape(
        coords.shape[0], tiles, TILE_POINTS
    )
    kern = near_kernels(tile_coords, pair_rows, pair_cols)
    scales = 2.0 ** ((1.0 - jnp.arange(levels, dtype=jnp.float32)) / 2.0)

    def near_of(values):
        tile_vec = values[:, perm].reshape(columns, tiles, TILE_POINTS)
        near_t = near_apply(kern, tile_vec, pair_rows, pair_cols).reshape(columns, points)
        return near_t[:, inverse]

    def sums_with_norm(values):
        proj = jnp.einsum("lp,cp,rp->lcr", level_gain, values, basis, precision=highest)
        norm = jnp.sum(values * values, axis=1)
        extra = jnp.broadcast_to(norm[None, :, None], (1, columns, rank))
        running = tree_sums(jnp.concatenate([proj, extra], axis=0))
        return running[:levels], running[levels, :, 0]

    solution = jnp.zeros_like(right_side)
    residual = right_side
    direction = right_side
    for step in range(ITERATIONS):
        if step == 0:
            nodesum, norm_now = sums_with_norm(residual)
            near = near_of(direction)
        else:
            residual_sum, norm_next = sums_with_norm(residual)
            residual_near = near_of(residual)
            ratio = norm_next / norm_now
            direction = residual + ratio[:, None] * direction
            nodesum = residual_sum + ratio[None, :, None] * nodesum
            near = residual_near + ratio[:, None] * near
            norm_now = norm_next
        coupled = jnp.einsum("lcr,lrs->lcs", nodesum, coupling, precision=highest)
        coupled = (
            jnp.einsum("lcs,lrs->lcr", coupled, coupling, precision=highest) * scales[:, None, None]
        )
        back = jnp.einsum("lcr,rp->lcp", coupled, basis, precision=highest)
        far = jnp.sum(back * level_gain[:, None, :], axis=0)
        image = noise[None, :] * direction + far + near
        curve = butterfly(jnp.sum(direction * image, axis=1))
        alpha = norm_now / curve
        solution = solution + alpha[:, None] * direction
        residual = residual - alpha[:, None] * image
    return (solution, residual)


def solution(mesh):
    return jax.shard_map(
        per_device,
        mesh=mesh,
        in_specs=(
            P(None, ("gx", "gy")),
            P(),
            P(("gx", "gy")),
            P(None, ("gx", "gy")),
            P(None, ("gx", "gy")),
            P(None, ("gx", "gy")),
            P(),
            P(("gx", "gy"), None),
            P(("gx", "gy"), None, None),
        ),
        out_specs=(P(None, ("gx", "gy")), P(None, ("gx", "gy"))),
        check_vma=False,
    )
```

```python
import math

import jax
import jax.numpy as jnp
from jax import lax
from jax.sharding import PartitionSpec as P

TILE_POINTS = 256
ITERATIONS = 2


near_weight = 0.25
highest = lax.Precision.HIGHEST


def swapped(value, axis, bit):
    mask = 2**bit
    pairs = [(source, source ^ mask) for source in range(lax.axis_size(axis))]
    return lax.ppermute(value, axis, pairs)


def near_kernels(tile_coords, pair_rows, pair_cols):
    union = jnp.concatenate([tile_coords[:, pair_rows], tile_coords[:, pair_cols]], axis=2)
    gram = jnp.einsum("fgi,fgj->gij", union, union, precision=highest)
    square = jnp.sum(union * union, axis=0)
    dist = square[:, :, None] + square[:, None, :] - 2.0 * gram
    return near_weight * jnp.exp(-0.5 * dist)


def near_apply(kern, tile_vec, pair_rows, pair_cols):
    width = tile_vec.shape[2]
    union_vec = jnp.concatenate([tile_vec[:, pair_rows], tile_vec[:, pair_cols]], axis=2)
    result = jnp.einsum("gij,cgj->cgi", kern, union_vec, precision=highest)
    tile_ids = jnp.arange(tile_vec.shape[1], dtype=jnp.int32)
    row_hot = (pair_rows[:, None] == tile_ids[None, :]).astype(jnp.float32)
    col_hot = (pair_cols[:, None] == tile_ids[None, :]).astype(jnp.float32)
    added = jnp.einsum("cgi,gt->cti", result[:, :, :width], row_hot, precision=highest)
    return added + jnp.einsum("cgi,gt->cti", result[:, :, width:], col_hot, precision=highest)


def tree_sums(proj):
    low_count = lax.axis_size("gy").bit_length() - 1
    high_count = lax.axis_size("gx").bit_length() - 1
    running = proj
    for bit in range(low_count):
        partner = swapped(running[bit:], "gy", bit)
        running = jnp.concatenate([running[:bit], running[bit:] + partner], axis=0)
    for bit in range(high_count):
        level = low_count + bit
        partner = swapped(running[level:], "gx", bit)
        running = jnp.concatenate([running[:level], running[level:] + partner], axis=0)
    return running


def butterfly(value):
    for bit in range(lax.axis_size("gy").bit_length() - 1):
        value = value + swapped(value, "gy", bit)
    for bit in range(lax.axis_size("gx").bit_length() - 1):
        value = value + swapped(value, "gx", bit)
    return value


def per_device(coords, inv_scale, noise, right_side, basis, level_gain, coupling, order, pairs):
    perm = order[0]
    columns, points = right_side.shape
    features = coords.shape[0]
    tiles = points // TILE_POINTS
    levels = level_gain.shape[0]
    rank = basis.shape[0]
    pair_rows = pairs[0, 0]
    pair_cols = pairs[0, 1]
    position = jnp.arange(points, dtype=jnp.int32)
    inverse = jnp.sum(jnp.where(perm[:, None] == position[None, :], position[:, None], 0), axis=0)
    stacked = jnp.concatenate([coords * inv_scale[:, None], right_side], axis=0)[:, perm]
    tile_coords = stacked[:features].reshape(features, tiles, TILE_POINTS)
    kern = near_kernels(tile_coords, pair_rows, pair_cols)
    scales = 2.0 ** ((1.0 - jnp.arange(levels, dtype=jnp.float32)) / 2.0)

    def near_tiles(values_t):
        tile_vec = values_t.reshape(columns, tiles, TILE_POINTS)
        return near_apply(kern, tile_vec, pair_rows, pair_cols).reshape(columns, points)

    def sums_with_norm(values):
        proj = jnp.einsum("lp,cp,rp->lcr", level_gain, values, basis, precision=highest)
        norm = jnp.sum(values * values, axis=1)
        extra = jnp.broadcast_to(norm[None, :, None], (1, columns, rank))
        running = tree_sums(jnp.concatenate([proj, extra], axis=0))
        return running[:levels], running[levels, :, 0]

    solution = jnp.zeros_like(right_side)
    residual = right_side
    direction = right_side
    direction_t = stacked[features:]
    for step in range(ITERATIONS):
        if step == 0:
            nodesum, norm_now = sums_with_norm(residual)
            near_t = near_tiles(direction_t)
            late_t, nodesum = lax.optimization_barrier((near_t, nodesum))
            near = late_t[:, inverse]
        else:
            residual_sum, norm_next = sums_with_norm(residual)
            residual_t = residual[:, perm]
            residual_near_t = near_tiles(residual_t)
            late_t, residual_sum = lax.optimization_barrier((residual_near_t, residual_sum))
            ratio = norm_next / norm_now
            direction = residual + ratio[:, None] * direction
            direction_t = residual_t + ratio[:, None] * direction_t
            nodesum = residual_sum + ratio[None, :, None] * nodesum
            near_t = residual_near_t + ratio[:, None] * near_t
            near = late_t[:, inverse] + ratio[:, None] * near
            norm_now = norm_next
        coupled = jnp.einsum("lcr,lrs->lcs", nodesum, coupling, precision=highest)
        coupled = (
            jnp.einsum("lcs,lrs->lcr", coupled, coupling, precision=highest) * scales[:, None, None]
        )
        back = jnp.einsum("lcr,rp->lcp", coupled, basis, precision=highest)
        far = jnp.sum(back * level_gain[:, None, :], axis=0)
        base = noise[None, :] * direction + far
        local = jnp.sum(direction * base, axis=1) + jnp.sum(direction_t * near_t, axis=1)
        curve = butterfly(local)
        alpha = norm_now / curve
        solution = solution + alpha[:, None] * direction
        residual = residual - alpha[:, None] * (base + near)
    return (solution, residual)


def solution(mesh):
    return jax.shard_map(
        per_device,
        mesh=mesh,
        in_specs=(
            P(None, ("gx", "gy")),
            P(),
            P(("gx", "gy")),
            P(None, ("gx", "gy")),
            P(None, ("gx", "gy")),
            P(None, ("gx", "gy")),
            P(),
            P(("gx", "gy"), None),
            P(("gx", "gy"), None, None),
        ),
        out_specs=(P(None, ("gx", "gy")), P(None, ("gx", "gy"))),
        check_vma=False,
    )
```

```python
import math

import jax
import jax.numpy as jnp
from jax import lax
from jax.sharding import PartitionSpec as P

TILE_POINTS = 256
ITERATIONS = 2


near_weight = 0.25
highest = lax.Precision.HIGHEST


def swapped(value, axis, bit):
    mask = 2**bit
    pairs = [(source, source ^ mask) for source in range(lax.axis_size(axis))]
    return lax.ppermute(value, axis, pairs)


def near_kernels(tile_coords, pair_rows, pair_cols):
    union = jnp.concatenate([tile_coords[:, pair_rows], tile_coords[:, pair_cols]], axis=2)
    gram = jnp.einsum("fgi,fgj->gij", union, union, precision=highest)
    square = jnp.sum(union * union, axis=0)
    dist = square[:, :, None] + square[:, None, :] - 2.0 * gram
    return near_weight * jnp.exp(-0.5 * dist)


def near_apply(kern, tile_vec, pair_rows, pair_cols):
    width = tile_vec.shape[2]
    union_vec = jnp.concatenate([tile_vec[:, pair_rows], tile_vec[:, pair_cols]], axis=2)
    result = jnp.einsum("gij,cgj->cgi", kern, union_vec, precision=highest)
    tile_ids = jnp.arange(tile_vec.shape[1], dtype=jnp.int32)
    row_hot = (pair_rows[:, None] == tile_ids[None, :]).astype(jnp.float32)
    col_hot = (pair_cols[:, None] == tile_ids[None, :]).astype(jnp.float32)
    added = jnp.einsum("cgi,gt->cti", result[:, :, :width], row_hot, precision=highest)
    return added + jnp.einsum("cgi,gt->cti", result[:, :, width:], col_hot, precision=highest)


def pieces(values):
    high = lax.reduce_precision(values, exponent_bits=8, mantissa_bits=7)
    rest = values - high
    middle = lax.reduce_precision(rest, exponent_bits=8, mantissa_bits=7)
    return jnp.concatenate([high, middle, rest - middle], axis=0).astype(jnp.bfloat16)


def select(values, hot, spec):
    count = values.shape[0]
    out = jnp.einsum(spec, pieces(values), hot, preferred_element_type=jnp.float32)
    return (out[:count] + out[count : 2 * count]) + out[2 * count :]


def tree_sums(proj):
    low_count = lax.axis_size("gy").bit_length() - 1
    high_count = lax.axis_size("gx").bit_length() - 1
    running = proj
    for bit in range(low_count):
        partner = swapped(running[bit:], "gy", bit)
        running = jnp.concatenate([running[:bit], running[bit:] + partner], axis=0)
    for bit in range(high_count):
        level = low_count + bit
        partner = swapped(running[level:], "gx", bit)
        running = jnp.concatenate([running[:level], running[level:] + partner], axis=0)
    return running


def butterfly(value):
    for bit in range(lax.axis_size("gy").bit_length() - 1):
        value = value + swapped(value, "gy", bit)
    for bit in range(lax.axis_size("gx").bit_length() - 1):
        value = value + swapped(value, "gx", bit)
    return value


def per_device(coords, inv_scale, noise, right_side, basis, level_gain, coupling, order, pairs):
    perm = order[0]
    columns, points = right_side.shape
    features = coords.shape[0]
    tiles = points // TILE_POINTS
    levels = level_gain.shape[0]
    rank = basis.shape[0]
    pair_rows = pairs[0, 0]
    pair_cols = pairs[0, 1]
    position = jnp.arange(points, dtype=jnp.int32)
    hot = (perm[:, None] == position[None, :]).astype(jnp.bfloat16)
    hot = hot.reshape(tiles, TILE_POINTS, points)
    stacked = select(jnp.concatenate([coords * inv_scale[:, None], right_side], axis=0), hot, "cp,ktp->ckt")
    tile_coords = stacked[:features]
    kern = lax.optimization_barrier(near_kernels(tile_coords, pair_rows, pair_cols))
    scales = 2.0 ** ((1.0 - jnp.arange(levels, dtype=jnp.float32)) / 2.0)

    def near_tiles(values_t):
        return near_apply(kern, values_t, pair_rows, pair_cols)

    def sums_with_norm(values):
        proj = jnp.einsum("lp,cp,rp->lcr", level_gain, values, basis, precision=highest)
        norm = jnp.sum(values * values, axis=1)
        extra = jnp.broadcast_to(norm[None, :, None], (1, columns, rank))
        running = tree_sums(jnp.concatenate([proj, extra], axis=0))
        return running[:levels], running[levels, :, 0]

    solution = jnp.zeros_like(right_side)
    residual = right_side
    direction = right_side
    direction_t = stacked[features:]
    for step in range(ITERATIONS):
        if step == 0:
            nodesum, norm_now = sums_with_norm(residual)
            near_t = near_tiles(direction_t)
            late_t, nodesum = lax.optimization_barrier((near_t, nodesum))
            near = select(late_t, hot, "ckt,ktp->cp")
        else:
            residual_sum, norm_next = sums_with_norm(residual)
            residual_t = select(residual, hot, "cp,ktp->ckt")
            residual_near_t = near_tiles(residual_t)
            late_t, residual_sum = lax.optimization_barrier((residual_near_t, residual_sum))
            ratio = norm_next / norm_now
            direction = residual + ratio[:, None] * direction
            direction_t = residual_t + ratio[:, None, None] * direction_t
            nodesum = residual_sum + ratio[None, :, None] * nodesum
            near_t = residual_near_t + ratio[:, None, None] * near_t
            near = select(late_t, hot, "ckt,ktp->cp") + ratio[:, None] * near
            norm_now = norm_next
        coupled = jnp.einsum("lcr,lrs->lcs", nodesum, coupling, precision=highest)
        coupled = (
            jnp.einsum("lcs,lrs->lcr", coupled, coupling, precision=highest) * scales[:, None, None]
        )
        back = jnp.einsum("lcr,rp->lcp", coupled, basis, precision=highest)
        far = jnp.sum(back * level_gain[:, None, :], axis=0)
        base = noise[None, :] * direction + far
        local = jnp.sum(direction * base, axis=1) + jnp.sum(direction_t * near_t, axis=(1, 2))
        curve = butterfly(local)
        alpha = norm_now / curve
        solution = solution + alpha[:, None] * direction
        residual = residual - alpha[:, None] * (base + near)
    return (solution, residual)


def solution(mesh):
    return jax.shard_map(
        per_device,
        mesh=mesh,
        in_specs=(
            P(None, ("gx", "gy")),
            P(),
            P(("gx", "gy")),
            P(None, ("gx", "gy")),
            P(None, ("gx", "gy")),
            P(None, ("gx", "gy")),
            P(),
            P(("gx", "gy"), None),
            P(("gx", "gy"), None, None),
        ),
        out_specs=(P(None, ("gx", "gy")), P(None, ("gx", "gy"))),
        check_vma=False,
    )
```

```python
import math

import jax
import jax.numpy as jnp
from jax import lax
from jax.sharding import PartitionSpec as P

TILE_POINTS = 256
ITERATIONS = 2


near_weight = 0.25
highest = lax.Precision.HIGHEST


def swapped(value, axis, bit):
    mask = 2**bit
    pairs = [(source, source ^ mask) for source in range(lax.axis_size(axis))]
    return lax.ppermute(value, axis, pairs)


def near_kernels(tile_coords, pair_rows, pair_cols):
    union = jnp.concatenate([tile_coords[pair_rows], tile_coords[pair_cols]], axis=2)
    gram = jnp.einsum("gfi,gfj->gij", union, union, precision=highest)
    square = jnp.sum(union * union, axis=1)
    dist = square[:, :, None] + square[:, None, :] - 2.0 * gram
    return near_weight * jnp.exp(-0.5 * dist)


def near_apply(kern, tile_vec, pair_rows, pair_cols):
    width = tile_vec.shape[2]
    union_vec = jnp.concatenate([tile_vec[pair_rows], tile_vec[pair_cols]], axis=2)
    result = jnp.einsum("gij,gcj->gci", kern, union_vec, precision=highest)
    tile_ids = jnp.arange(tile_vec.shape[0], dtype=jnp.int32)
    row_hot = (pair_rows[:, None] == tile_ids[None, :]).astype(jnp.float32)
    col_hot = (pair_cols[:, None] == tile_ids[None, :]).astype(jnp.float32)
    added = jnp.einsum("gci,gk->kci", result[:, :, :width], row_hot, precision=highest)
    return added + jnp.einsum("gci,gk->kci", result[:, :, width:], col_hot, precision=highest)


def pieces(values, axis):
    high = lax.reduce_precision(values, exponent_bits=8, mantissa_bits=7)
    rest = values - high
    middle = lax.reduce_precision(rest, exponent_bits=8, mantissa_bits=7)
    return jnp.concatenate([high, middle, rest - middle], axis=axis).astype(jnp.bfloat16)


def to_tiles(values, hot):
    count = values.shape[0]
    out = jnp.einsum("cp,ktp->kct", pieces(values, 0), hot, preferred_element_type=jnp.float32)
    return (out[:, :count] + out[:, count : 2 * count]) + out[:, 2 * count :]


def to_points(values_t, hot):
    count = values_t.shape[1]
    out = jnp.einsum("kct,ktp->cp", pieces(values_t, 1), hot, preferred_element_type=jnp.float32)
    return (out[:count] + out[count : 2 * count]) + out[2 * count :]


def tree_sums(proj):
    low_count = lax.axis_size("gy").bit_length() - 1
    high_count = lax.axis_size("gx").bit_length() - 1
    running = proj
    for bit in range(low_count):
        partner = swapped(running[bit:], "gy", bit)
        running = jnp.concatenate([running[:bit], running[bit:] + partner], axis=0)
    for bit in range(high_count):
        level = low_count + bit
        partner = swapped(running[level:], "gx", bit)
        running = jnp.concatenate([running[:level], running[level:] + partner], axis=0)
    return running


def butterfly(value):
    for bit in range(lax.axis_size("gy").bit_length() - 1):
        value = value + swapped(value, "gy", bit)
    for bit in range(lax.axis_size("gx").bit_length() - 1):
        value = value + swapped(value, "gx", bit)
    return value


def per_device(coords, inv_scale, noise, right_side, basis, level_gain, coupling, order, pairs):
    perm = order.reshape(order.shape[1])
    columns, points = right_side.shape
    features = coords.shape[0]
    tiles = points // TILE_POINTS
    levels = level_gain.shape[0]
    rank = basis.shape[0]
    pair_rows = pairs[0, 0]
    pair_cols = pairs[0, 1]
    position = jnp.arange(points, dtype=jnp.int32)
    hot = (perm[:, None] == position[None, :]).astype(jnp.bfloat16)
    hot = hot.reshape(tiles, TILE_POINTS, points)
    stacked = to_tiles(jnp.concatenate([coords * inv_scale[:, None], right_side], axis=0), hot)
    tile_coords = stacked[:, :features]
    kern = lax.optimization_barrier(near_kernels(tile_coords, pair_rows, pair_cols))
    scales = 2.0 ** ((1.0 - jnp.arange(levels, dtype=jnp.float32)) / 2.0)

    def near_tiles(values_t):
        return near_apply(kern, values_t, pair_rows, pair_cols)

    def sums_with_norm(values):
        proj = jnp.einsum("lp,cp,rp->lcr", level_gain, values, basis, precision=highest)
        norm = jnp.sum(values * values, axis=1)
        extra = jnp.broadcast_to(norm[None, :, None], (1, columns, rank))
        running = tree_sums(jnp.concatenate([proj, extra], axis=0))
        return running[:levels], running[levels, :, 0]

    solution = jnp.zeros_like(right_side)
    residual = right_side
    direction = right_side
    direction_t = stacked[:, features:]
    for step in range(ITERATIONS):
        if step == 0:
            nodesum, norm_now = sums_with_norm(residual)
            near_t = near_tiles(direction_t)
            late_t, nodesum = lax.optimization_barrier((near_t, nodesum))
            near = to_points(late_t, hot)
        else:
            residual_sum, norm_next = sums_with_norm(residual)
            residual_t = to_tiles(residual, hot)
            residual_near_t = near_tiles(residual_t)
            late_t, residual_sum = lax.optimization_barrier((residual_near_t, residual_sum))
            ratio = norm_next / norm_now
            direction = residual + ratio[:, None] * direction
            direction_t = residual_t + ratio[None, :, None] * direction_t
            nodesum = residual_sum + ratio[None, :, None] * nodesum
            near_t = residual_near_t + ratio[None, :, None] * near_t
            near = to_points(late_t, hot) + ratio[:, None] * near
            norm_now = norm_next
        coupled = jnp.einsum("lcr,lrs->lcs", nodesum, coupling, precision=highest)
        coupled = (
            jnp.einsum("lcs,lrs->lcr", coupled, coupling, precision=highest) * scales[:, None, None]
        )
        back = jnp.einsum("lcr,rp->lcp", coupled, basis, precision=highest)
        far = jnp.sum(back * level_gain[:, None, :], axis=0)
        base = noise[None, :] * direction + far
        local = jnp.sum(direction * base, axis=1) + jnp.sum(direction_t * near_t, axis=(0, 2))
        curve = butterfly(local)
        alpha = norm_now / curve
        solution = solution + alpha[:, None] * direction
        residual = residual - alpha[:, None] * (base + near)
    return (solution, residual)


def solution(mesh):
    return jax.shard_map(
        per_device,
        mesh=mesh,
        in_specs=(
            P(None, ("gx", "gy")),
            P(),
            P(("gx", "gy")),
            P(None, ("gx", "gy")),
            P(None, ("gx", "gy")),
            P(None, ("gx", "gy")),
            P(),
            P(("gx", "gy"), None),
            P(("gx", "gy"), None, None),
        ),
        out_specs=(P(None, ("gx", "gy")), P(None, ("gx", "gy"))),
        check_vma=False,
    )
```

```python
import math

import jax
import jax.numpy as jnp
from jax import lax
from jax.sharding import PartitionSpec as P

TILE_POINTS = 256
ITERATIONS = 2


near_weight = 0.25
highest = lax.Precision.HIGHEST


def swapped(value, axis, bit):
    mask = 2**bit
    pairs = [(source, source ^ mask) for source in range(lax.axis_size(axis))]
    return lax.ppermute(value, axis, pairs)


def near_kernels(tile_coords, pair_rows, pair_cols):
    union = jnp.concatenate([tile_coords[pair_rows], tile_coords[pair_cols]], axis=2)
    gram = jnp.einsum("gfi,gfj->gij", union, union, precision=highest)
    square = jnp.sum(union * union, axis=1)
    dist = square[:, :, None] + square[:, None, :] - 2.0 * gram
    return near_weight * jnp.exp(-0.5 * dist)


def near_apply(kern, tile_vec, pair_rows, pair_cols):
    width = tile_vec.shape[2]
    union_vec = jnp.concatenate([tile_vec[pair_rows], tile_vec[pair_cols]], axis=2)
    result = jnp.einsum("gij,gcj->gci", kern, union_vec, precision=highest)
    tile_ids = jnp.arange(tile_vec.shape[0], dtype=jnp.int32)
    row_hot = (pair_rows[:, None] == tile_ids[None, :]).astype(jnp.float32)
    col_hot = (pair_cols[:, None] == tile_ids[None, :]).astype(jnp.float32)
    added = jnp.einsum("gci,gk->kci", result[:, :, :width], row_hot, precision=highest)
    return added + jnp.einsum("gci,gk->kci", result[:, :, width:], col_hot, precision=highest)


def pieces(values, axis):
    high = lax.reduce_precision(values, exponent_bits=8, mantissa_bits=7)
    rest = values - high
    middle = lax.reduce_precision(rest, exponent_bits=8, mantissa_bits=7)
    return jnp.concatenate([high, middle, rest - middle], axis=axis).astype(jnp.bfloat16)


def to_tiles(values, hot):
    count = values.shape[0]
    out = jnp.einsum("cp,ktp->kct", pieces(values, 0), hot, preferred_element_type=jnp.float32)
    return (out[:, :count] + out[:, count : 2 * count]) + out[:, 2 * count :]


def to_points(values_t, hot):
    count = values_t.shape[1]
    out = jnp.einsum("kct,ktp->cp", pieces(values_t, 1), hot, preferred_element_type=jnp.float32)
    return (out[:count] + out[count : 2 * count]) + out[2 * count :]


def tree_sums(proj, stages, state):
    low_count = lax.axis_size("gy").bit_length() - 1
    high_count = lax.axis_size("gx").bit_length() - 1
    rounds = [("gy", bit, bit) for bit in range(low_count)]
    rounds += [("gx", bit, low_count + bit) for bit in range(high_count)]
    running = proj
    for index, (axis, bit, level) in enumerate(rounds):
        partner = swapped(running[level:], axis, bit)
        if index < len(stages):
            state, running = lax.optimization_barrier((state, running))
            state = stages[index](state)
        running = jnp.concatenate([running[:level], running[level:] + partner], axis=0)
        if index < len(stages):
            running, state = lax.optimization_barrier((running, state))
    for stage in stages[len(rounds) :]:
        state = stage(state)
    return running, state


def butterfly(value):
    for bit in range(lax.axis_size("gy").bit_length() - 1):
        value = value + swapped(value, "gy", bit)
    for bit in range(lax.axis_size("gx").bit_length() - 1):
        value = value + swapped(value, "gx", bit)
    return value


def per_device(coords, inv_scale, noise, right_side, basis, level_gain, coupling, order, pairs):
    perm = order.reshape(order.shape[1])
    columns, points = right_side.shape
    features = coords.shape[0]
    tiles = points // TILE_POINTS
    levels = level_gain.shape[0]
    rank = basis.shape[0]
    pair_rows = pairs[0, 0]
    pair_cols = pairs[0, 1]
    position = jnp.arange(points, dtype=jnp.int32)
    hot = (perm[:, None] == position[None, :]).astype(jnp.bfloat16)
    hot = hot.reshape(tiles, TILE_POINTS, points)
    scales = 2.0 ** ((1.0 - jnp.arange(levels, dtype=jnp.float32)) / 2.0)

    def sums_with_norm(values, stages, state):
        proj = jnp.einsum("lp,cp,rp->lcr", level_gain, values, basis, precision=highest)
        norm = jnp.sum(values * values, axis=1)
        extra = jnp.broadcast_to(norm[None, :, None], (1, columns, rank))
        running, state = tree_sums(jnp.concatenate([proj, extra], axis=0), stages, state)
        return running[:levels], running[levels, :, 0], state

    def permute_inputs(unused):
        stacked = to_tiles(jnp.concatenate([coords * inv_scale[:, None], right_side], axis=0), hot)
        return stacked[:, :features], stacked[:, features:]

    def kernel_blocks(state):
        tile_coords, direction_t = state
        return near_kernels(tile_coords, pair_rows, pair_cols), direction_t

    def first_near(state):
        kern, direction_t = state
        return kern, direction_t, near_apply(kern, direction_t, pair_rows, pair_cols)

    def permute_residual(state):
        kern, values = state
        return kern, to_tiles(values, hot)

    def residual_near(state):
        kern, values_t = state
        return values_t, near_apply(kern, values_t, pair_rows, pair_cols)

    solution = jnp.zeros_like(right_side)
    residual = right_side
    direction = right_side
    for step in range(ITERATIONS):
        if step == 0:
            stages = [permute_inputs, kernel_blocks, first_near]
            nodesum, norm_now, (kern, direction_t, near_t) = sums_with_norm(
                residual, stages, jnp.zeros((), jnp.float32)
            )
            late_t, nodesum = lax.optimization_barrier((near_t, nodesum))
            near = to_points(late_t, hot)
        else:
            stages = [permute_residual, residual_near]
            residual_sum, norm_next, (residual_t, residual_near_t) = sums_with_norm(
                residual, stages, (kern, residual)
            )
            late_t, residual_sum = lax.optimization_barrier((residual_near_t, residual_sum))
            ratio = norm_next / norm_now
            direction = residual + ratio[:, None] * direction
            direction_t = residual_t + ratio[None, :, None] * direction_t
            nodesum = residual_sum + ratio[None, :, None] * nodesum
            near_t = residual_near_t + ratio[None, :, None] * near_t
            near = to_points(late_t, hot) + ratio[:, None] * near
            norm_now = norm_next
        coupled = jnp.einsum("lcr,lrs->lcs", nodesum, coupling, precision=highest)
        coupled = (
            jnp.einsum("lcs,lrs->lcr", coupled, coupling, precision=highest) * scales[:, None, None]
        )
        back = jnp.einsum("lcr,rp->lcp", coupled, basis, precision=highest)
        far = jnp.sum(back * level_gain[:, None, :], axis=0)
        base = noise[None, :] * direction + far
        local = jnp.sum(direction * base, axis=1) + jnp.sum(direction_t * near_t, axis=(0, 2))
        curve = butterfly(local)
        alpha = norm_now / curve
        solution = solution + alpha[:, None] * direction
        residual = residual - alpha[:, None] * (base + near)
    return (solution, residual)


def solution(mesh):
    return jax.shard_map(
        per_device,
        mesh=mesh,
        in_specs=(
            P(None, ("gx", "gy")),
            P(),
            P(("gx", "gy")),
            P(None, ("gx", "gy")),
            P(None, ("gx", "gy")),
            P(None, ("gx", "gy")),
            P(),
            P(("gx", "gy"), None),
            P(("gx", "gy"), None, None),
        ),
        out_specs=(P(None, ("gx", "gy")), P(None, ("gx", "gy"))),
        check_vma=False,
    )
```

```python
import math

import jax
import jax.numpy as jnp
from jax import lax
from jax.sharding import PartitionSpec as P

TILE_POINTS = 256
ITERATIONS = 2


near_weight = 0.25
highest = lax.Precision.HIGHEST


def swapped(value, axis, bit):
    mask = 2**bit
    pairs = [(source, source ^ mask) for source in range(lax.axis_size(axis))]
    return lax.ppermute(value, axis, pairs)


def pair_union(tiled, pair_rows, pair_cols):
    unions = []
    for pair in range(pair_rows.shape[0]):
        row = lax.dynamic_index_in_dim(tiled, pair_rows[pair], axis=0, keepdims=False)
        col = lax.dynamic_index_in_dim(tiled, pair_cols[pair], axis=0, keepdims=False)
        unions.append(jnp.concatenate([row, col], axis=1))
    return jnp.stack(unions, axis=0)


def near_kernels(tile_coords, pair_rows, pair_cols):
    union = pair_union(tile_coords, pair_rows, pair_cols)
    gram = jnp.einsum("gfi,gfj->gij", union, union, precision=highest)
    square = jnp.sum(union * union, axis=1)
    dist = square[:, :, None] + square[:, None, :] - 2.0 * gram
    return near_weight * jnp.exp(-0.5 * dist)


def near_apply(kern, tile_vec, pair_rows, pair_cols):
    width = tile_vec.shape[2]
    union_vec = pair_union(tile_vec, pair_rows, pair_cols)
    result = jnp.einsum("gij,gcj->gci", kern, union_vec, precision=lax.Precision.HIGH)
    tile_ids = jnp.arange(tile_vec.shape[0], dtype=jnp.int32)
    row_hot = (pair_rows[:, None] == tile_ids[None, :]).astype(jnp.float32)
    col_hot = (pair_cols[:, None] == tile_ids[None, :]).astype(jnp.float32)
    added = jnp.einsum("gci,gk->kci", result[:, :, :width], row_hot, precision=highest)
    return added + jnp.einsum("gci,gk->kci", result[:, :, width:], col_hot, precision=highest)


def pieces(values, axis):
    high = lax.reduce_precision(values, exponent_bits=8, mantissa_bits=7)
    rest = values - high
    middle = lax.reduce_precision(rest, exponent_bits=8, mantissa_bits=7)
    return jnp.concatenate([high, middle, rest - middle], axis=axis).astype(jnp.bfloat16)


def to_tiles(values, hot):
    count = values.shape[0]
    out = jnp.einsum("cp,ktp->kct", pieces(values, 0), hot, preferred_element_type=jnp.float32)
    return (out[:, :count] + out[:, count : 2 * count]) + out[:, 2 * count :]


def to_points(values_t, hot):
    count = values_t.shape[1]
    out = jnp.einsum("kct,ktp->cp", pieces(values_t, 1), hot, preferred_element_type=jnp.float32)
    return (out[:count] + out[count : 2 * count]) + out[2 * count :]


def tree_sums(proj):
    low_count = lax.axis_size("gy").bit_length() - 1
    high_count = lax.axis_size("gx").bit_length() - 1
    running = proj
    for bit in range(low_count):
        partner = swapped(running[bit:], "gy", bit)
        running = jnp.concatenate([running[:bit], running[bit:] + partner], axis=0)
    for bit in range(high_count):
        level = low_count + bit
        partner = swapped(running[level:], "gx", bit)
        running = jnp.concatenate([running[:level], running[level:] + partner], axis=0)
    return running


def butterfly(value):
    for bit in range(lax.axis_size("gy").bit_length() - 1):
        value = value + swapped(value, "gy", bit)
    for bit in range(lax.axis_size("gx").bit_length() - 1):
        value = value + swapped(value, "gx", bit)
    return value


def per_device(coords, inv_scale, noise, right_side, basis, level_gain, coupling, order, pairs):
    columns, points = right_side.shape
    features = coords.shape[0]
    tiles = points // TILE_POINTS
    levels = level_gain.shape[0]
    rank = basis.shape[0]
    pair_rows = pairs[0, 0]
    pair_cols = pairs[0, 1]
    position = jnp.arange(points, dtype=jnp.int32)
    hot = (jnp.transpose(order) == position[None, :]).astype(jnp.bfloat16)
    hot = hot.reshape(tiles, TILE_POINTS, points)
    stacked = to_tiles(jnp.concatenate([coords * inv_scale[:, None], right_side], axis=0), hot)
    tile_coords = stacked[:, :features]
    kern = lax.optimization_barrier(near_kernels(tile_coords, pair_rows, pair_cols))
    scales = 2.0 ** ((1.0 - jnp.arange(levels, dtype=jnp.float32)) / 2.0)

    def near_tiles(values_t):
        return near_apply(kern, values_t, pair_rows, pair_cols)

    def sums_with_norm(values):
        proj = jnp.einsum("lp,cp,rp->lcr", level_gain, values, basis, precision=highest)
        norm = jnp.sum(values * values, axis=1)
        extra = jnp.broadcast_to(norm[None, :, None], (1, columns, rank))
        running = tree_sums(jnp.concatenate([proj, extra], axis=0))
        return running[:levels], running[levels, :, 0]

    solution = jnp.zeros_like(right_side)
    residual = right_side
    direction = right_side
    direction_t = stacked[:, features:]
    for step in range(ITERATIONS):
        if step == 0:
            nodesum, norm_now = sums_with_norm(residual)
            near_t = near_tiles(direction_t)
            late_t, nodesum = lax.optimization_barrier((near_t, nodesum))
            near = to_points(late_t, hot)
        else:
            residual_sum, norm_next = sums_with_norm(residual)
            residual_t = to_tiles(residual, hot)
            residual_near_t = near_tiles(residual_t)
            late_t, residual_sum = lax.optimization_barrier((residual_near_t, residual_sum))
            ratio = norm_next / norm_now
            direction = residual + ratio[:, None] * direction
            direction_t = residual_t + ratio[None, :, None] * direction_t
            nodesum = residual_sum + ratio[None, :, None] * nodesum
            near_t = residual_near_t + ratio[None, :, None] * near_t
            near = to_points(late_t, hot) + ratio[:, None] * near
            norm_now = norm_next
        coupled = jnp.einsum("lcr,lrs->lcs", nodesum, coupling, precision=highest)
        coupled = (
            jnp.einsum("lcs,lrs->lcr", coupled, coupling, precision=highest) * scales[:, None, None]
        )
        back = jnp.einsum("lcr,rp->lcp", coupled, basis, precision=highest)
        far = jnp.sum(back * level_gain[:, None, :], axis=0)
        base = noise[None, :] * direction + far
        local = jnp.sum(direction * base, axis=1) + jnp.sum(direction_t * near_t, axis=(0, 2))
        curve = butterfly(local)
        alpha = norm_now / curve
        solution = solution + alpha[:, None] * direction
        residual = residual - alpha[:, None] * (base + near)
    return (solution, residual)


def solution(mesh):
    return jax.shard_map(
        per_device,
        mesh=mesh,
        in_specs=(
            P(None, ("gx", "gy")),
            P(),
            P(("gx", "gy")),
            P(None, ("gx", "gy")),
            P(None, ("gx", "gy")),
            P(None, ("gx", "gy")),
            P(),
            P(("gx", "gy"), None),
            P(("gx", "gy"), None, None),
        ),
        out_specs=(P(None, ("gx", "gy")), P(None, ("gx", "gy"))),
        check_vma=False,
    )
```

```python
import math

import jax
import jax.numpy as jnp
from jax import lax
from jax.sharding import PartitionSpec as P

TILE_POINTS = 256
ITERATIONS = 2


near_weight = 0.25
highest = lax.Precision.HIGHEST


def swapped(value, axis, bit):
    mask = 2**bit
    pairs = [(source, source ^ mask) for source in range(lax.axis_size(axis))]
    return lax.ppermute(value, axis, pairs)


def near_kernels(union):
    gram = jnp.einsum("gfi,gfj->gij", union, union, precision=highest)
    square = jnp.sum(union * union, axis=1)
    dist = square[:, :, None] + square[:, None, :] - 2.0 * gram
    return near_weight * jnp.exp(-0.5 * dist)


def near_apply(kern, union_vec):
    return jnp.einsum("gij,gcj->gci", kern, union_vec, precision=lax.Precision.HIGH)


def pieces(values, axis):
    high = lax.reduce_precision(values, exponent_bits=8, mantissa_bits=7)
    rest = values - high
    middle = lax.reduce_precision(rest, exponent_bits=8, mantissa_bits=7)
    return jnp.concatenate([high, middle, rest - middle], axis=axis).astype(jnp.bfloat16)


def to_union(values, hot):
    count = values.shape[0]
    out = jnp.einsum("cp,gip->gci", pieces(values, 0), hot, preferred_element_type=jnp.float32)
    return (out[:, :count] + out[:, count : 2 * count]) + out[:, 2 * count :]


def from_union(values_u, hot):
    count = values_u.shape[1]
    out = jnp.einsum("gci,gip->cp", pieces(values_u, 1), hot, preferred_element_type=jnp.float32)
    return (out[:count] + out[count : 2 * count]) + out[2 * count :]


def tree_sums(proj):
    low_count = lax.axis_size("gy").bit_length() - 1
    high_count = lax.axis_size("gx").bit_length() - 1
    running = proj
    for bit in range(low_count):
        partner = swapped(running[bit:], "gy", bit)
        running = jnp.concatenate([running[:bit], running[bit:] + partner], axis=0)
    for bit in range(high_count):
        level = low_count + bit
        partner = swapped(running[level:], "gx", bit)
        running = jnp.concatenate([running[:level], running[level:] + partner], axis=0)
    return running


def butterfly(value):
    for bit in range(lax.axis_size("gy").bit_length() - 1):
        value = value + swapped(value, "gy", bit)
    for bit in range(lax.axis_size("gx").bit_length() - 1):
        value = value + swapped(value, "gx", bit)
    return value


def per_device(coords, inv_scale, noise, right_side, basis, level_gain, coupling, order, pairs):
    columns, points = right_side.shape
    features = coords.shape[0]
    tiles = points // TILE_POINTS
    levels = level_gain.shape[0]
    rank = basis.shape[0]
    order_tiles = order.reshape(tiles, TILE_POINTS)
    union_order = jnp.concatenate([order_tiles[pairs[0, 0]], order_tiles[pairs[0, 1]]], axis=1)
    position = jnp.arange(points, dtype=jnp.int32)
    hot = (union_order[:, :, None] == position[None, None, :]).astype(jnp.bfloat16)
    stacked = to_union(jnp.concatenate([coords * inv_scale[:, None], right_side], axis=0), hot)
    kern = lax.optimization_barrier(near_kernels(stacked[:, :features]))
    scales = 2.0 ** ((1.0 - jnp.arange(levels, dtype=jnp.float32)) / 2.0)

    def near_of_union(values_u):
        return near_apply(kern, values_u)

    def sums_with_norm(values):
        proj = jnp.einsum("lp,cp,rp->lcr", level_gain, values, basis, precision=highest)
        norm = jnp.sum(values * values, axis=1)
        extra = jnp.broadcast_to(norm[None, :, None], (1, columns, rank))
        running = tree_sums(jnp.concatenate([proj, extra], axis=0))
        return running[:levels], running[levels, :, 0]

    solution = jnp.zeros_like(right_side)
    residual = right_side
    direction = right_side
    direction_u = stacked[:, features:]
    for step in range(ITERATIONS):
        if step == 0:
            nodesum, norm_now = sums_with_norm(residual)
            near_u = near_of_union(direction_u)
            late_u, nodesum = lax.optimization_barrier((near_u, nodesum))
            near = from_union(late_u, hot)
        else:
            residual_sum, norm_next = sums_with_norm(residual)
            residual_u = to_union(residual, hot)
            residual_near_u = near_of_union(residual_u)
            late_u, residual_sum = lax.optimization_barrier((residual_near_u, residual_sum))
            ratio = norm_next / norm_now
            direction = residual + ratio[:, None] * direction
            direction_u = residual_u + ratio[None, :, None] * direction_u
            nodesum = residual_sum + ratio[None, :, None] * nodesum
            near_u = residual_near_u + ratio[None, :, None] * near_u
            near = from_union(late_u, hot) + ratio[:, None] * near
            norm_now = norm_next
        coupled = jnp.einsum("lcr,lrs->lcs", nodesum, coupling, precision=highest)
        coupled = (
            jnp.einsum("lcs,lrs->lcr", coupled, coupling, precision=highest) * scales[:, None, None]
        )
        back = jnp.einsum("lcr,rp->lcp", coupled, basis, precision=highest)
        far = jnp.sum(back * level_gain[:, None, :], axis=0)
        base = noise[None, :] * direction + far
        local = jnp.sum(direction * base, axis=1) + jnp.sum(direction_u * near_u, axis=(0, 2))
        curve = butterfly(local)
        alpha = norm_now / curve
        solution = solution + alpha[:, None] * direction
        residual = residual - alpha[:, None] * (base + near)
    return (solution, residual)


def solution(mesh):
    return jax.shard_map(
        per_device,
        mesh=mesh,
        in_specs=(
            P(None, ("gx", "gy")),
            P(),
            P(("gx", "gy")),
            P(None, ("gx", "gy")),
            P(None, ("gx", "gy")),
            P(None, ("gx", "gy")),
            P(),
            P(("gx", "gy"), None),
            P(("gx", "gy"), None, None),
        ),
        out_specs=(P(None, ("gx", "gy")), P(None, ("gx", "gy"))),
        check_vma=False,
    )
```

```python
import math

import jax
import jax.numpy as jnp
from jax import lax
from jax.sharding import PartitionSpec as P

TILE_POINTS = 256
ITERATIONS = 2


near_weight = 0.25
highest = lax.Precision.HIGHEST


def swapped(value, axis, bit):
    mask = 2**bit
    pairs = [(source, source ^ mask) for source in range(lax.axis_size(axis))]
    return lax.ppermute(value, axis, pairs)


def near_kernels(union):
    gram = jnp.einsum("gfi,gfj->gij", union, union, precision=highest)
    square = jnp.sum(union * union, axis=1)
    dist = square[:, :, None] + square[:, None, :] - 2.0 * gram
    return near_weight * jnp.exp(-0.5 * dist)


def near_apply(kern, union_vec):
    return jnp.einsum("gij,gcj->gci", kern, union_vec, precision=lax.Precision.HIGH)


def pieces(values, axis):
    high = lax.reduce_precision(values, exponent_bits=8, mantissa_bits=7)
    rest = values - high
    middle = lax.reduce_precision(rest, exponent_bits=8, mantissa_bits=7)
    return jnp.concatenate([high, middle, rest - middle], axis=axis).astype(jnp.bfloat16)


def to_union(values, hot):
    count = values.shape[0]
    out = jnp.einsum("cp,gip->gci", pieces(values, 0), hot, preferred_element_type=jnp.float32)
    return (out[:, :count] + out[:, count : 2 * count]) + out[:, 2 * count :]


def from_union(values_u, hot):
    count = values_u.shape[1]
    out = jnp.einsum("gci,gip->cp", pieces(values_u, 1), hot, preferred_element_type=jnp.float32)
    return (out[:count] + out[count : 2 * count]) + out[2 * count :]


def tree_sums(proj):
    low_count = lax.axis_size("gy").bit_length() - 1
    high_count = lax.axis_size("gx").bit_length() - 1
    running = proj
    for bit in range(low_count):
        partner = swapped(running[bit:], "gy", bit)
        running = jnp.concatenate([running[:bit], running[bit:] + partner], axis=0)
    for bit in range(high_count):
        level = low_count + bit
        partner = swapped(running[level:], "gx", bit)
        running = jnp.concatenate([running[:level], running[level:] + partner], axis=0)
    return running


def butterfly(value):
    for bit in range(lax.axis_size("gy").bit_length() - 1):
        value = value + swapped(value, "gy", bit)
    for bit in range(lax.axis_size("gx").bit_length() - 1):
        value = value + swapped(value, "gx", bit)
    return value


def per_device(coords, inv_scale, noise, right_side, basis, level_gain, coupling, order, pairs):
    columns, points = right_side.shape
    features = coords.shape[0]
    tiles = points // TILE_POINTS
    levels = level_gain.shape[0]
    rank = basis.shape[0]
    order_tiles = order.reshape(tiles, TILE_POINTS)
    union_order = jnp.concatenate([order_tiles[pairs[0, 0]], order_tiles[pairs[0, 1]]], axis=1)
    position = jnp.arange(points, dtype=jnp.int32)
    hot = (union_order[:, :, None] == position[None, None, :]).astype(jnp.bfloat16)
    stacked = to_union(jnp.concatenate([coords * inv_scale[:, None], right_side], axis=0), hot)
    kern = lax.optimization_barrier(near_kernels(stacked[:, :features]))
    scales = 2.0 ** ((1.0 - jnp.arange(levels, dtype=jnp.float32)) / 2.0)

    def near_of_union(values_u):
        return lax.optimization_barrier(near_apply(kern, values_u))

    def sums_with_norm(values):
        proj = jnp.einsum("lp,cp,rp->lcr", level_gain, values, basis, precision=highest)
        norm = jnp.sum(values * values, axis=1)
        extra = jnp.broadcast_to(norm[None, :, None], (1, columns, rank))
        running = tree_sums(jnp.concatenate([proj, extra], axis=0))
        return running[:levels], running[levels, :, 0]

    solution = jnp.zeros_like(right_side)
    residual = right_side
    direction = right_side
    direction_u = stacked[:, features:]
    for step in range(ITERATIONS):
        if step == 0:
            nodesum, norm_now = sums_with_norm(residual)
            near_u = near_of_union(direction_u)
            late_u, nodesum = lax.optimization_barrier((near_u, nodesum))
            near = from_union(late_u, hot)
        else:
            residual_sum, norm_next = sums_with_norm(residual)
            residual_u = to_union(residual, hot)
            residual_near_u = near_of_union(residual_u)
            late_u, residual_sum = lax.optimization_barrier((residual_near_u, residual_sum))
            ratio = norm_next / norm_now
            direction = residual + ratio[:, None] * direction
            direction_u = residual_u + ratio[None, :, None] * direction_u
            nodesum = residual_sum + ratio[None, :, None] * nodesum
            near_u = residual_near_u + ratio[None, :, None] * near_u
            near = from_union(late_u, hot) + ratio[:, None] * near
            norm_now = norm_next
        coupled = jnp.einsum("lcr,lrs->lcs", nodesum, coupling, precision=highest)
        coupled = (
            jnp.einsum("lcs,lrs->lcr", coupled, coupling, precision=highest) * scales[:, None, None]
        )
        back = jnp.einsum("lcr,rp->lcp", coupled, basis, precision=highest)
        far = jnp.sum(back * level_gain[:, None, :], axis=0)
        base = noise[None, :] * direction + far
        local = jnp.sum(direction * base, axis=1) + jnp.sum(direction_u * near_u, axis=(0, 2))
        curve = butterfly(local)
        alpha = norm_now / curve
        solution = solution + alpha[:, None] * direction
        residual = residual - alpha[:, None] * (base + near)
    return (solution, residual)


def solution(mesh):
    return jax.shard_map(
        per_device,
        mesh=mesh,
        in_specs=(
            P(None, ("gx", "gy")),
            P(),
            P(("gx", "gy")),
            P(None, ("gx", "gy")),
            P(None, ("gx", "gy")),
            P(None, ("gx", "gy")),
            P(),
            P(("gx", "gy"), None),
            P(("gx", "gy"), None, None),
        ),
        out_specs=(P(None, ("gx", "gy")), P(None, ("gx", "gy"))),
        check_vma=False,
    )
```

```python
import math

import jax
import jax.numpy as jnp
from jax import lax
from jax.sharding import PartitionSpec as P

TILE_POINTS = 256
ITERATIONS = 2


near_weight = 0.25
highest = lax.Precision.HIGHEST


def swapped(value, axis, bit):
    mask = 2**bit
    pairs = [(source, source ^ mask) for source in range(lax.axis_size(axis))]
    return lax.ppermute(value, axis, pairs)


def split3(values):
    high = lax.reduce_precision(values, exponent_bits=8, mantissa_bits=7)
    rest = values - high
    middle = lax.reduce_precision(rest, exponent_bits=8, mantissa_bits=7)
    return high, middle, rest - middle


def near_kernels(union):
    high, middle, low = split3(union)
    left = jnp.concatenate([high, high, middle, high, low, middle], axis=1).astype(jnp.bfloat16)
    right = jnp.concatenate([high, middle, high, low, high, middle], axis=1).astype(jnp.bfloat16)
    gram = jnp.einsum("gfi,gfj->gij", left, right, preferred_element_type=jnp.float32)
    square = jnp.sum(union * union, axis=1)
    dist = square[:, :, None] + square[:, None, :] - 2.0 * gram
    return near_weight * jnp.exp(-0.5 * dist)


def near_apply(kern, union_vec):
    return jnp.einsum("gij,gcj->gci", kern, union_vec, precision=lax.Precision.HIGH)


def pieces(values, axis):
    return jnp.concatenate(split3(values), axis=axis).astype(jnp.bfloat16)


def to_union(values, hot):
    count = values.shape[0]
    out = jnp.einsum("cp,gip->gci", pieces(values, 0), hot, preferred_element_type=jnp.float32)
    return (out[:, :count] + out[:, count : 2 * count]) + out[:, 2 * count :]


def from_union(values_u, hot):
    count = values_u.shape[1]
    out = jnp.einsum("gci,gip->cp", pieces(values_u, 1), hot, preferred_element_type=jnp.float32)
    return (out[:count] + out[count : 2 * count]) + out[2 * count :]


def tree_sums(proj):
    low_count = lax.axis_size("gy").bit_length() - 1
    high_count = lax.axis_size("gx").bit_length() - 1
    running = proj
    for bit in range(low_count):
        partner = swapped(running[bit:], "gy", bit)
        running = jnp.concatenate([running[:bit], running[bit:] + partner], axis=0)
    for bit in range(high_count):
        level = low_count + bit
        partner = swapped(running[level:], "gx", bit)
        running = jnp.concatenate([running[:level], running[level:] + partner], axis=0)
    return running


def butterfly(value):
    for bit in range(lax.axis_size("gy").bit_length() - 1):
        value = value + swapped(value, "gy", bit)
    for bit in range(lax.axis_size("gx").bit_length() - 1):
        value = value + swapped(value, "gx", bit)
    return value


def per_device(coords, inv_scale, noise, right_side, basis, level_gain, coupling, order, pairs):
    columns, points = right_side.shape
    features = coords.shape[0]
    tiles = points // TILE_POINTS
    levels = level_gain.shape[0]
    rank = basis.shape[0]
    order_tiles = order.reshape(tiles, TILE_POINTS)
    union_order = jnp.concatenate([order_tiles[pairs[0, 0]], order_tiles[pairs[0, 1]]], axis=1)
    position = jnp.arange(points, dtype=jnp.int32)
    hot = (union_order[:, :, None] == position[None, None, :]).astype(jnp.bfloat16)
    stacked = to_union(jnp.concatenate([coords, right_side], axis=0), hot)
    kern = lax.optimization_barrier(near_kernels(stacked[:, :features] * inv_scale[None, :, None]))
    scales = 2.0 ** ((1.0 - jnp.arange(levels, dtype=jnp.float32)) / 2.0)

    def near_of_union(values_u):
        return lax.optimization_barrier(near_apply(kern, values_u))

    def sums_with_norm(values):
        proj = jnp.einsum("lp,cp,rp->lcr", level_gain, values, basis, precision=highest)
        norm = jnp.sum(values * values, axis=1)
        extra = jnp.broadcast_to(norm[None, :, None], (1, columns, rank))
        running = tree_sums(jnp.concatenate([proj, extra], axis=0))
        return running[:levels], running[levels, :, 0]

    solution = jnp.zeros_like(right_side)
    residual = right_side
    direction = right_side
    direction_u = stacked[:, features:]
    for step in range(ITERATIONS):
        if step == 0:
            nodesum, norm_now = sums_with_norm(residual)
            near_u = near_of_union(direction_u)
            late_u, nodesum = lax.optimization_barrier((near_u, nodesum))
            near = from_union(late_u, hot)
        else:
            residual_sum, norm_next = sums_with_norm(residual)
            residual_u = to_union(residual, hot)
            residual_near_u = near_of_union(residual_u)
            late_u, residual_sum = lax.optimization_barrier((residual_near_u, residual_sum))
            ratio = norm_next / norm_now
            direction = residual + ratio[:, None] * direction
            direction_u = residual_u + ratio[None, :, None] * direction_u
            nodesum = residual_sum + ratio[None, :, None] * nodesum
            near_u = residual_near_u + ratio[None, :, None] * near_u
            near = from_union(late_u, hot) + ratio[:, None] * near
            norm_now = norm_next
        coupled = jnp.einsum("lcr,lrs->lcs", nodesum, coupling, precision=highest)
        coupled = (
            jnp.einsum("lcs,lrs->lcr", coupled, coupling, precision=highest) * scales[:, None, None]
        )
        back = jnp.einsum("lcr,rp->lcp", coupled, basis, precision=highest)
        far = jnp.sum(back * level_gain[:, None, :], axis=0)
        base = noise[None, :] * direction + far
        local = jnp.sum(direction * base, axis=1) + jnp.sum(direction_u * near_u, axis=(0, 2))
        curve = butterfly(local)
        alpha = norm_now / curve
        solution = solution + alpha[:, None] * direction
        residual = residual - alpha[:, None] * (base + near)
    return (solution, residual)


def solution(mesh):
    return jax.shard_map(
        per_device,
        mesh=mesh,
        in_specs=(
            P(None, ("gx", "gy")),
            P(),
            P(("gx", "gy")),
            P(None, ("gx", "gy")),
            P(None, ("gx", "gy")),
            P(None, ("gx", "gy")),
            P(),
            P(("gx", "gy"), None),
            P(("gx", "gy"), None, None),
        ),
        out_specs=(P(None, ("gx", "gy")), P(None, ("gx", "gy"))),
        check_vma=False,
    )
```

```python
import math

import jax
import jax.numpy as jnp
from jax import lax
from jax.sharding import PartitionSpec as P

TILE_POINTS = 256
ITERATIONS = 2


near_weight = 0.25
highest = lax.Precision.HIGHEST


def swapped(value, axis, bit):
    mask = 2**bit
    pairs = [(source, source ^ mask) for source in range(lax.axis_size(axis))]
    return lax.ppermute(value, axis, pairs)


def split3(values):
    high = lax.reduce_precision(values, exponent_bits=8, mantissa_bits=7)
    rest = values - high
    middle = lax.reduce_precision(rest, exponent_bits=8, mantissa_bits=7)
    return high, middle, rest - middle


def near_kernels(union):
    high, middle, low = split3(union)
    left = jnp.concatenate([high, high, middle, high, low, middle], axis=1).astype(jnp.bfloat16)
    right = jnp.concatenate([high, middle, high, low, high, middle], axis=1).astype(jnp.bfloat16)
    gram = jnp.einsum("gfi,gfj->gij", left, right, preferred_element_type=jnp.float32)
    square = jnp.sum(union * union, axis=1)
    dist = square[:, :, None] + square[:, None, :] - 2.0 * gram
    return near_weight * jnp.exp(-0.5 * dist)


def near_apply(kern, union_vec):
    return jnp.einsum("gij,gcj->gci", kern, union_vec, precision=lax.Precision.HIGH)


def pieces(values, axis):
    return jnp.concatenate(split3(values), axis=axis).astype(jnp.bfloat16)


def to_union(values, hot):
    count = values.shape[0]
    out = jnp.einsum("cp,gip->gci", pieces(values, 0), hot, preferred_element_type=jnp.float32)
    return (out[:, :count] + out[:, count : 2 * count]) + out[:, 2 * count :]


def from_union(values_u, hot):
    count = values_u.shape[1]
    out = jnp.einsum("gci,gip->cp", pieces(values_u, 1), hot, preferred_element_type=jnp.float32)
    return (out[:count] + out[count : 2 * count]) + out[2 * count :]


def tree_sums(proj):
    low_count = lax.axis_size("gy").bit_length() - 1
    high_count = lax.axis_size("gx").bit_length() - 1
    running = proj
    for bit in range(low_count):
        partner = swapped(running[bit:], "gy", bit)
        running = jnp.concatenate([running[:bit], running[bit:] + partner], axis=0)
    for bit in range(high_count):
        level = low_count + bit
        partner = swapped(running[level:], "gx", bit)
        running = jnp.concatenate([running[:level], running[level:] + partner], axis=0)
    return running


def butterfly(value, stages, state):
    rounds = [("gy", bit) for bit in range(lax.axis_size("gy").bit_length() - 1)]
    rounds += [("gx", bit) for bit in range(lax.axis_size("gx").bit_length() - 1)]
    for index, (axis, bit) in enumerate(rounds):
        partner = swapped(value, axis, bit)
        if index < len(stages):
            state, value = lax.optimization_barrier((state, value))
            state = stages[index](state)
        value = value + partner
        if index < len(stages):
            value, state = lax.optimization_barrier((value, state))
    for stage in stages[len(rounds) :]:
        state = stage(state)
    return value, state


def per_device(coords, inv_scale, noise, right_side, basis, level_gain, coupling, order, pairs):
    columns, points = right_side.shape
    features = coords.shape[0]
    tiles = points // TILE_POINTS
    levels = level_gain.shape[0]
    rank = basis.shape[0]
    order_tiles = order.reshape(tiles, TILE_POINTS)
    union_order = jnp.concatenate([order_tiles[pairs[0, 0]], order_tiles[pairs[0, 1]]], axis=1)
    position = jnp.arange(points, dtype=jnp.int32)
    hot = (union_order[:, :, None] == position[None, None, :]).astype(jnp.bfloat16)
    stacked = to_union(jnp.concatenate([coords, right_side], axis=0), hot)
    kern = lax.optimization_barrier(near_kernels(stacked[:, :features] * inv_scale[None, :, None]))
    scales = 2.0 ** ((1.0 - jnp.arange(levels, dtype=jnp.float32)) / 2.0)

    def near_of_union(values_u):
        return lax.optimization_barrier(near_apply(kern, values_u))

    def project(values):
        return jnp.einsum("lp,cp,rp->lcr", level_gain, values, basis, precision=highest)

    def sums_with_norm(values, proj):
        norm = jnp.sum(values * values, axis=1)
        extra = jnp.broadcast_to(norm[None, :, None], (1, columns, rank))
        running = tree_sums(jnp.concatenate([proj, extra], axis=0))
        return running[:levels], running[levels, :, 0]

    half = union_order.shape[0] // 2

    def unpermute_first(state):
        late, near, extra = state
        return late, from_union(late[:half], hot[:half]) + extra, extra

    def unpermute_second(state):
        late, near, extra = state
        return late, near + from_union(late[half:], hot[half:]), extra

    solution = jnp.zeros_like(right_side)
    residual = right_side
    direction = right_side
    direction_u = stacked[:, features:]
    residual_proj = project(residual)
    for step in range(ITERATIONS):
        if step == 0:
            nodesum, norm_now = sums_with_norm(residual, residual_proj)
            near_u = near_of_union(direction_u)
            late_u, nodesum = lax.optimization_barrier((near_u, nodesum))
            carried = jnp.zeros_like(right_side)
        else:
            residual_sum, norm_next = sums_with_norm(residual, residual_proj)
            residual_u = to_union(residual, hot)
            residual_near_u = near_of_union(residual_u)
            late_u, residual_sum = lax.optimization_barrier((residual_near_u, residual_sum))
            ratio = norm_next / norm_now
            direction = residual + ratio[:, None] * direction
            direction_u = residual_u + ratio[None, :, None] * direction_u
            nodesum = residual_sum + ratio[None, :, None] * nodesum
            near_u = residual_near_u + ratio[None, :, None] * near_u
            carried = ratio[:, None] * near
            norm_now = norm_next
        coupled = jnp.einsum("lcr,lrs->lcs", nodesum, coupling, precision=highest)
        coupled = (
            jnp.einsum("lcs,lrs->lcr", coupled, coupling, precision=highest) * scales[:, None, None]
        )
        back = jnp.einsum("lcr,rp->lcp", coupled, basis, precision=highest)
        far = jnp.sum(back * level_gain[:, None, :], axis=0)
        base = noise[None, :] * direction + far
        local = jnp.sum(direction * base, axis=1) + jnp.sum(direction_u * near_u, axis=(0, 2))
        def project_image(state, base=base):
            late, near, extra = state
            return late, near, project(base + near)

        stages = [unpermute_first, unpermute_second]
        if step + 1 < ITERATIONS:
            stages.append(project_image)
        curve, (late_u, near, image_proj) = butterfly(local, stages, (late_u, carried, carried))
        alpha = norm_now / curve
        solution = solution + alpha[:, None] * direction
        residual = residual - alpha[:, None] * (base + near)
        if step + 1 < ITERATIONS:
            residual_proj = residual_proj - alpha[None, :, None] * image_proj
    return (solution, residual)


def solution(mesh):
    return jax.shard_map(
        per_device,
        mesh=mesh,
        in_specs=(
            P(None, ("gx", "gy")),
            P(),
            P(("gx", "gy")),
            P(None, ("gx", "gy")),
            P(None, ("gx", "gy")),
            P(None, ("gx", "gy")),
            P(),
            P(("gx", "gy"), None),
            P(("gx", "gy"), None, None),
        ),
        out_specs=(P(None, ("gx", "gy")), P(None, ("gx", "gy"))),
        check_vma=False,
    )
```

```python
import math

import jax
import jax.numpy as jnp
from jax import lax
from jax.sharding import PartitionSpec as P

TILE_POINTS = 256
ITERATIONS = 2


near_weight = 0.25
highest = lax.Precision.HIGHEST


def swapped(value, axis, bit):
    mask = 2**bit
    pairs = [(source, source ^ mask) for source in range(lax.axis_size(axis))]
    return lax.ppermute(value, axis, pairs)


def split3(values):
    high = lax.reduce_precision(values, exponent_bits=8, mantissa_bits=7)
    rest = values - high
    middle = lax.reduce_precision(rest, exponent_bits=8, mantissa_bits=7)
    return high, middle, rest - middle


def near_kernels(union):
    high, middle, low = split3(union)
    left = jnp.concatenate([high, high, middle, high, low, middle], axis=1).astype(jnp.bfloat16)
    right = jnp.concatenate([high, middle, high, low, high, middle], axis=1).astype(jnp.bfloat16)
    gram = jnp.einsum("gfi,gfj->gij", left, right, preferred_element_type=jnp.float32)
    square = jnp.sum(union * union, axis=1)
    dist = square[:, :, None] + square[:, None, :] - 2.0 * gram
    return near_weight * jnp.exp(-0.5 * dist)


def near_apply(kern, union_vec):
    return jnp.einsum("gij,gcj->gci", kern, union_vec, precision=lax.Precision.HIGH)


def pieces(values, axis):
    return jnp.concatenate(split3(values), axis=axis).astype(jnp.bfloat16)


def to_union(values, hot):
    count = values.shape[0]
    out = jnp.einsum("cp,gip->gci", pieces(values, 0), hot, preferred_element_type=jnp.float32)
    return (out[:, :count] + out[:, count : 2 * count]) + out[:, 2 * count :]


def from_union(values_u, hot):
    count = values_u.shape[1]
    out = jnp.einsum("gci,gip->cp", pieces(values_u, 1), hot, preferred_element_type=jnp.float32)
    return (out[:count] + out[count : 2 * count]) + out[2 * count :]


def tree_sums(proj):
    low_count = lax.axis_size("gy").bit_length() - 1
    high_count = lax.axis_size("gx").bit_length() - 1
    running = proj
    for bit in range(low_count):
        partner = swapped(running[bit:], "gy", bit)
        running = jnp.concatenate([running[:bit], running[bit:] + partner], axis=0)
    for bit in range(high_count):
        level = low_count + bit
        partner = swapped(running[level:], "gx", bit)
        running = jnp.concatenate([running[:level], running[level:] + partner], axis=0)
    return running


def butterfly(value, stages, state):
    rounds = [("gy", bit) for bit in range(lax.axis_size("gy").bit_length() - 1)]
    rounds += [("gx", bit) for bit in range(lax.axis_size("gx").bit_length() - 1)]
    for index, (axis, bit) in enumerate(rounds):
        partner = swapped(value, axis, bit)
        if index < len(stages):
            state, value = lax.optimization_barrier((state, value))
            state = stages[index](state)
        value = value + partner
        if index < len(stages):
            value, state = lax.optimization_barrier((value, state))
    for stage in stages[len(rounds) :]:
        state = stage(state)
    return value, state


def per_device(coords, inv_scale, noise, right_side, basis, level_gain, coupling, order, pairs):
    columns, points = right_side.shape
    features = coords.shape[0]
    tiles = points // TILE_POINTS
    levels = level_gain.shape[0]
    rank = basis.shape[0]
    order_tiles = order.reshape(tiles, TILE_POINTS)
    union_order = jnp.concatenate([order_tiles[pairs[0, 0]], order_tiles[pairs[0, 1]]], axis=1)
    position = jnp.arange(points, dtype=jnp.int32)
    hot = (union_order[:, :, None] == position[None, None, :]).astype(jnp.bfloat16)
    stacked = to_union(jnp.concatenate([coords, right_side], axis=0), hot)
    kern = lax.optimization_barrier(near_kernels(stacked[:, :features] * inv_scale[None, :, None]))
    scales = 2.0 ** ((1.0 - jnp.arange(levels, dtype=jnp.float32)) / 2.0)

    def near_of_union(values_u):
        return lax.optimization_barrier(near_apply(kern, values_u))

    def project(values):
        return jnp.einsum("lp,cp,rp->lcr", level_gain, values, basis, precision=highest)

    def sums_with_norm(values, proj):
        norm = jnp.sum(values * values, axis=1)
        extra = jnp.broadcast_to(norm[None, :, None], (1, columns, rank))
        running = tree_sums(jnp.concatenate([proj, extra], axis=0))
        return running[:levels], running[levels, :, 0]

    half = union_order.shape[0] // 2
    hot_first = (union_order[:half, :, None] == position[None, None, :]).astype(jnp.bfloat16)
    hot_second = (union_order[half:, :, None] == position[None, None, :]).astype(jnp.bfloat16)

    def unpermute_first(state):
        late, near, extra = state
        return late, from_union(late[:half], hot_first) + extra, extra

    def unpermute_second(state):
        late, near, extra = state
        return late, near + from_union(late[half:], hot_second), extra

    solution = jnp.zeros_like(right_side)
    residual = right_side
    direction = right_side
    direction_u = stacked[:, features:]
    residual_proj = project(residual)
    for step in range(ITERATIONS):
        if step == 0:
            nodesum, norm_now = sums_with_norm(residual, residual_proj)
            near_u = near_of_union(direction_u)
            late_u, nodesum = lax.optimization_barrier((near_u, nodesum))
            carried = jnp.zeros_like(right_side)
        else:
            residual_sum, norm_next = sums_with_norm(residual, residual_proj)
            residual_u = to_union(residual, hot)
            residual_near_u = near_of_union(residual_u)
            late_u, residual_sum = lax.optimization_barrier((residual_near_u, residual_sum))
            ratio = norm_next / norm_now
            direction = residual + ratio[:, None] * direction
            direction_u = residual_u + ratio[None, :, None] * direction_u
            nodesum = residual_sum + ratio[None, :, None] * nodesum
            near_u = residual_near_u + ratio[None, :, None] * near_u
            carried = ratio[:, None] * near
            norm_now = norm_next
        coupled = jnp.einsum("lcr,lrs->lcs", nodesum, coupling, precision=highest)
        coupled = (
            jnp.einsum("lcs,lrs->lcr", coupled, coupling, precision=highest) * scales[:, None, None]
        )
        back = jnp.einsum("lcr,rp->lcp", coupled, basis, precision=highest)
        far = jnp.sum(back * level_gain[:, None, :], axis=0)
        base = noise[None, :] * direction + far
        local = jnp.sum(direction * base, axis=1) + jnp.sum(direction_u * near_u, axis=(0, 2))
        def project_image(state, base=base):
            late, near, extra = state
            return late, near, project(base + near)

        stages = [unpermute_first, unpermute_second]
        if step + 1 < ITERATIONS:
            stages.append(project_image)
        curve, (late_u, near, image_proj) = butterfly(local, stages, (late_u, carried, carried))
        alpha = norm_now / curve
        solution = solution + alpha[:, None] * direction
        residual = residual - alpha[:, None] * (base + near)
        if step + 1 < ITERATIONS:
            residual_proj = residual_proj - alpha[None, :, None] * image_proj
    return (solution, residual)


def solution(mesh):
    return jax.shard_map(
        per_device,
        mesh=mesh,
        in_specs=(
            P(None, ("gx", "gy")),
            P(),
            P(("gx", "gy")),
            P(None, ("gx", "gy")),
            P(None, ("gx", "gy")),
            P(None, ("gx", "gy")),
            P(),
            P(("gx", "gy"), None),
            P(("gx", "gy"), None, None),
        ),
        out_specs=(P(None, ("gx", "gy")), P(None, ("gx", "gy"))),
        check_vma=False,
    )
```

```python
import math

import jax
import jax.numpy as jnp
from jax import lax
from jax.sharding import PartitionSpec as P

TILE_POINTS = 256
ITERATIONS = 2


near_weight = 0.25
highest = lax.Precision.HIGHEST


def swapped(value, axis, bit):
    mask = 2**bit
    pairs = [(source, source ^ mask) for source in range(lax.axis_size(axis))]
    return lax.ppermute(value, axis, pairs)


def split3(values):
    high = lax.reduce_precision(values, exponent_bits=8, mantissa_bits=7)
    rest = values - high
    middle = lax.reduce_precision(rest, exponent_bits=8, mantissa_bits=7)
    return high, middle, rest - middle


def near_kernels(union):
    high, middle, low = split3(union)
    left = jnp.concatenate([high, high, middle, high, low, middle], axis=1).astype(jnp.bfloat16)
    right = jnp.concatenate([high, middle, high, low, high, middle], axis=1).astype(jnp.bfloat16)
    gram = jnp.einsum("gfi,gfj->gij", left, right, preferred_element_type=jnp.float32)
    square = jnp.sum(union * union, axis=1)
    dist = square[:, :, None] + square[:, None, :] - 2.0 * gram
    return near_weight * jnp.exp(-0.5 * dist)


def near_apply(kern, union_vec):
    return jnp.einsum("gij,gcj->gci", kern, union_vec, precision=lax.Precision.HIGH)


def pieces(values, axis):
    return jnp.concatenate(split3(values), axis=axis).astype(jnp.bfloat16)


def to_union(values, hot):
    count = values.shape[0]
    out = jnp.einsum("cp,gip->gci", pieces(values, 0), hot, preferred_element_type=jnp.float32)
    return (out[:, :count] + out[:, count : 2 * count]) + out[:, 2 * count :]


def from_union(values_u, hot):
    count = values_u.shape[1]
    out = jnp.einsum("gci,gip->cp", pieces(values_u, 1), hot, preferred_element_type=jnp.float32)
    return (out[:count] + out[count : 2 * count]) + out[2 * count :]


def tree_sums(proj, stages, state):
    low_count = lax.axis_size("gy").bit_length() - 1
    high_count = lax.axis_size("gx").bit_length() - 1
    rounds = [("gy", bit, bit) for bit in range(low_count)]
    rounds += [("gx", bit, low_count + bit) for bit in range(high_count)]
    running = proj
    for index, (axis, bit, level) in enumerate(rounds):
        partner = swapped(running[level:], axis, bit)
        stage = stages[index] if index < len(stages) else None
        if stage is not None:
            state, running = lax.optimization_barrier((state, running))
            state = stage(state)
        running = jnp.concatenate([running[:level], running[level:] + partner], axis=0)
        if stage is not None:
            running, state = lax.optimization_barrier((running, state))
    for stage in stages[len(rounds) :]:
        if stage is not None:
            state = stage(state)
    return running, state


def butterfly(value, stages, state):
    rounds = [("gy", bit) for bit in range(lax.axis_size("gy").bit_length() - 1)]
    rounds += [("gx", bit) for bit in range(lax.axis_size("gx").bit_length() - 1)]
    for index, (axis, bit) in enumerate(rounds):
        partner = swapped(value, axis, bit)
        if index < len(stages):
            state, value = lax.optimization_barrier((state, value))
            state = stages[index](state)
        value = value + partner
        if index < len(stages):
            value, state = lax.optimization_barrier((value, state))
    for stage in stages[len(rounds) :]:
        state = stage(state)
    return value, state


def per_device(coords, inv_scale, noise, right_side, basis, level_gain, coupling, order, pairs):
    columns, points = right_side.shape
    features = coords.shape[0]
    tiles = points // TILE_POINTS
    levels = level_gain.shape[0]
    rank = basis.shape[0]
    order_tiles = order.reshape(tiles, TILE_POINTS)
    union_order = jnp.concatenate([order_tiles[pairs[0, 0]], order_tiles[pairs[0, 1]]], axis=1)
    position = jnp.arange(points, dtype=jnp.int32)
    hot = (union_order[:, :, None] == position[None, None, :]).astype(jnp.bfloat16)
    stacked = to_union(jnp.concatenate([coords, right_side], axis=0), hot)
    kern = lax.optimization_barrier(near_kernels(stacked[:, :features] * inv_scale[None, :, None]))
    scales = 2.0 ** ((1.0 - jnp.arange(levels, dtype=jnp.float32)) / 2.0)

    def near_of_union(values_u):
        return lax.optimization_barrier(near_apply(kern, values_u))

    def project(values):
        return jnp.einsum("lp,cp,rp->lcr", level_gain, values, basis, precision=highest)

    def sums_with_norm(values, proj, stages, state):
        norm = jnp.sum(values * values, axis=1)
        extra = jnp.broadcast_to(norm[None, :, None], (1, columns, rank))
        running, state = tree_sums(jnp.concatenate([proj, extra], axis=0), stages, state)
        return running[:levels], running[levels, :, 0], state

    def permute_first(state):
        values, first, second = state
        return values, to_union(values, hot_first), second

    def permute_second(state):
        values, first, second = state
        return values, first, to_union(values, hot_second)

    def near_of_halves(state):
        values, first, second = state
        values_u = jnp.concatenate([first, second], axis=0)
        return values_u, near_of_union(values_u), second

    half = union_order.shape[0] // 2
    hot_first = (union_order[:half, :, None] == position[None, None, :]).astype(jnp.bfloat16)
    hot_second = (union_order[half:, :, None] == position[None, None, :]).astype(jnp.bfloat16)

    def unpermute_first(state):
        late, near, extra = state
        return late, from_union(late[:half], hot_first) + extra, extra

    def unpermute_second(state):
        late, near, extra = state
        return late, near + from_union(late[half:], hot_second), extra

    solution = jnp.zeros_like(right_side)
    residual = right_side
    direction = right_side
    direction_u = stacked[:, features:]
    residual_proj = project(residual)
    for step in range(ITERATIONS):
        if step == 0:
            nodesum, norm_now, unused = sums_with_norm(residual, residual_proj, [], ())
            near_u = near_of_union(direction_u)
            late_u, nodesum = lax.optimization_barrier((near_u, nodesum))
            carried = jnp.zeros_like(right_side)
        else:
            empty = jnp.zeros((half,) + direction_u.shape[1:], jnp.float32)
            stages = [permute_first, permute_second, None, near_of_halves]
            residual_sum, norm_next, (residual_u, residual_near_u, unused) = sums_with_norm(
                residual, residual_proj, stages, (residual, empty, empty)
            )
            late_u, residual_sum = lax.optimization_barrier((residual_near_u, residual_sum))
            ratio = norm_next / norm_now
            direction = residual + ratio[:, None] * direction
            direction_u = residual_u + ratio[None, :, None] * direction_u
            nodesum = residual_sum + ratio[None, :, None] * nodesum
            near_u = residual_near_u + ratio[None, :, None] * near_u
            carried = ratio[:, None] * near
            norm_now = norm_next
        coupled = jnp.einsum("lcr,lrs->lcs", nodesum, coupling, precision=highest)
        coupled = (
            jnp.einsum("lcs,lrs->lcr", coupled, coupling, precision=highest) * scales[:, None, None]
        )
        back = jnp.einsum("lcr,rp->lcp", coupled, basis, precision=highest)
        far = jnp.sum(back * level_gain[:, None, :], axis=0)
        base = noise[None, :] * direction + far
        local = jnp.sum(direction * base, axis=1) + jnp.sum(direction_u * near_u, axis=(0, 2))
        def project_image(state, base=base):
            late, near, extra = state
            return late, near, project(base + near)

        stages = [unpermute_first, unpermute_second]
        if step + 1 < ITERATIONS:
            stages.append(project_image)
        curve, (late_u, near, image_proj) = butterfly(local, stages, (late_u, carried, carried))
        alpha = norm_now / curve
        solution = solution + alpha[:, None] * direction
        residual = residual - alpha[:, None] * (base + near)
        if step + 1 < ITERATIONS:
            residual_proj = residual_proj - alpha[None, :, None] * image_proj
    return (solution, residual)


def solution(mesh):
    return jax.shard_map(
        per_device,
        mesh=mesh,
        in_specs=(
            P(None, ("gx", "gy")),
            P(),
            P(("gx", "gy")),
            P(None, ("gx", "gy")),
            P(None, ("gx", "gy")),
            P(None, ("gx", "gy")),
            P(),
            P(("gx", "gy"), None),
            P(("gx", "gy"), None, None),
        ),
        out_specs=(P(None, ("gx", "gy")), P(None, ("gx", "gy"))),
        check_vma=False,
    )
```

```python
import math

import jax
import jax.numpy as jnp
from jax import lax
from jax.sharding import PartitionSpec as P

TILE_POINTS = 256
ITERATIONS = 2


near_weight = 0.25
highest = lax.Precision.HIGHEST


def swapped(value, axis, bit):
    mask = 2**bit
    pairs = [(source, source ^ mask) for source in range(lax.axis_size(axis))]
    return lax.ppermute(value, axis, pairs)


def split3(values):
    high = lax.reduce_precision(values, exponent_bits=8, mantissa_bits=7)
    rest = values - high
    middle = lax.reduce_precision(rest, exponent_bits=8, mantissa_bits=7)
    return high, middle, rest - middle


def near_kernels(union):
    high, middle, low = split3(union)
    left = jnp.concatenate([high, high, middle, high, low, middle], axis=1).astype(jnp.bfloat16)
    right = jnp.concatenate([high, middle, high, low, high, middle], axis=1).astype(jnp.bfloat16)
    gram = jnp.einsum("gfi,gfj->gij", left, right, preferred_element_type=jnp.float32)
    square = jnp.sum(union * union, axis=1)
    dist = square[:, :, None] + square[:, None, :] - 2.0 * gram
    return near_weight * jnp.exp(-0.5 * dist)


def near_apply(kern, union_vec):
    return jnp.einsum("gij,gcj->gci", kern, union_vec, precision=lax.Precision.HIGH)


def pieces(values, axis):
    return jnp.concatenate(split3(values), axis=axis).astype(jnp.bfloat16)


def to_union(values, hot):
    count = values.shape[0]
    out = jnp.einsum("cp,gip->gci", pieces(values, 0), hot, preferred_element_type=jnp.float32)
    return (out[:, :count] + out[:, count : 2 * count]) + out[:, 2 * count :]


def from_union(values_u, hot):
    count = values_u.shape[1]
    out = jnp.einsum("gci,gip->cp", pieces(values_u, 1), hot, preferred_element_type=jnp.float32)
    return (out[:count] + out[count : 2 * count]) + out[2 * count :]


def tree_sums(proj, stages, state):
    low_count = lax.axis_size("gy").bit_length() - 1
    high_count = lax.axis_size("gx").bit_length() - 1
    rounds = [("gy", bit, bit) for bit in range(low_count)]
    rounds += [("gx", bit, low_count + bit) for bit in range(high_count)]
    running = proj
    for index, (axis, bit, level) in enumerate(rounds):
        partner = swapped(running[level:], axis, bit)
        stage = stages[index] if index < len(stages) else None
        if stage is not None:
            state, running = lax.optimization_barrier((state, running))
            state = stage(state)
        running = jnp.concatenate([running[:level], running[level:] + partner], axis=0)
        if stage is not None:
            running, state = lax.optimization_barrier((running, state))
    for stage in stages[len(rounds) :]:
        if stage is not None:
            state = stage(state)
    return running, state


def butterfly(value, stages, state):
    rounds = [("gy", bit) for bit in range(lax.axis_size("gy").bit_length() - 1)]
    rounds += [("gx", bit) for bit in range(lax.axis_size("gx").bit_length() - 1)]
    for index, (axis, bit) in enumerate(rounds):
        partner = swapped(value, axis, bit)
        if index < len(stages):
            state, value = lax.optimization_barrier((state, value))
            state = stages[index](state)
        value = value + partner
        if index < len(stages):
            value, state = lax.optimization_barrier((value, state))
    for stage in stages[len(rounds) :]:
        state = stage(state)
    return value, state


def per_device(coords, inv_scale, noise, right_side, basis, level_gain, coupling, order, pairs):
    columns, points = right_side.shape
    features = coords.shape[0]
    tiles = points // TILE_POINTS
    levels = level_gain.shape[0]
    rank = basis.shape[0]
    order_tiles = order.reshape(tiles, TILE_POINTS)
    union_order = jnp.concatenate([order_tiles[pairs[0, 0]], order_tiles[pairs[0, 1]]], axis=1)
    position = jnp.arange(points, dtype=jnp.int32)
    hot = (union_order[:, :, None] == position[None, None, :]).astype(jnp.bfloat16)
    scales = 2.0 ** ((1.0 - jnp.arange(levels, dtype=jnp.float32)) / 2.0)


    def project(values):
        return jnp.einsum("lp,cp,rp->lcr", level_gain, values, basis, precision=highest)

    def sums_with_norm(values, proj, stages, state):
        norm = jnp.sum(values * values, axis=1)
        extra = jnp.broadcast_to(norm[None, :, None], (1, columns, rank))
        running, state = tree_sums(jnp.concatenate([proj, extra], axis=0), stages, state)
        return running[:levels], running[levels, :, 0], state

    def permute_first(state):
        values, first, second = state
        return values, to_union(values, hot_first), second

    def permute_second(state):
        values, first, second = state
        return values, first, to_union(values, hot_second)

    def near_of_halves(state):
        values, first, second = state
        values_u = jnp.concatenate([first, second], axis=0)
        return values_u, lax.optimization_barrier(near_apply(kern, values_u)), second

    half = union_order.shape[0] // 2
    hot_first = (union_order[:half, :, None] == position[None, None, :]).astype(jnp.bfloat16)
    hot_second = (union_order[half:, :, None] == position[None, None, :]).astype(jnp.bfloat16)

    def unpermute_first(state):
        late, near, extra = state
        return late, from_union(late[:half], hot_first) + extra, extra

    def unpermute_second(state):
        late, near, extra = state
        return late, near + from_union(late[half:], hot_second), extra

    def permute_inputs(unused):
        stacked = to_union(jnp.concatenate([coords, right_side], axis=0), hot)
        return stacked[:, :features] * inv_scale[None, :, None], stacked[:, features:]

    def kernel_blocks(state):
        union_coords, direction_u = state
        return near_kernels(union_coords), direction_u

    def first_near(state):
        kern, direction_u = state
        return kern, direction_u, lax.optimization_barrier(near_apply(kern, direction_u))

    solution = jnp.zeros_like(right_side)
    residual = right_side
    direction = right_side
    residual_proj = project(residual)
    for step in range(ITERATIONS):
        if step == 0:
            stages = [permute_inputs, kernel_blocks, None, first_near]
            nodesum, norm_now, (kern, direction_u, near_u) = sums_with_norm(
                residual, residual_proj, stages, jnp.zeros((), jnp.float32)
            )
            late_u, nodesum = lax.optimization_barrier((near_u, nodesum))
            carried = jnp.zeros_like(right_side)
        else:
            empty = jnp.zeros((half,) + direction_u.shape[1:], jnp.float32)
            stages = [permute_first, permute_second, None, near_of_halves]
            residual_sum, norm_next, (residual_u, residual_near_u, unused) = sums_with_norm(
                residual, residual_proj, stages, (residual, empty, empty)
            )
            late_u, residual_sum = lax.optimization_barrier((residual_near_u, residual_sum))
            ratio = norm_next / norm_now
            direction = residual + ratio[:, None] * direction
            direction_u = residual_u + ratio[None, :, None] * direction_u
            nodesum = residual_sum + ratio[None, :, None] * nodesum
            near_u = residual_near_u + ratio[None, :, None] * near_u
            carried = ratio[:, None] * near
            norm_now = norm_next
        coupled = jnp.einsum("lcr,lrs->lcs", nodesum, coupling, precision=highest)
        coupled = (
            jnp.einsum("lcs,lrs->lcr", coupled, coupling, precision=highest) * scales[:, None, None]
        )
        back = jnp.einsum("lcr,rp->lcp", coupled, basis, precision=highest)
        far = jnp.sum(back * level_gain[:, None, :], axis=0)
        base = noise[None, :] * direction + far
        local = jnp.sum(direction * base, axis=1) + jnp.sum(direction_u * near_u, axis=(0, 2))
        def project_image(state, base=base):
            late, near, extra = state
            return late, near, project(base + near)

        stages = [unpermute_first, unpermute_second]
        if step + 1 < ITERATIONS:
            stages.append(project_image)
        curve, (late_u, near, image_proj) = butterfly(local, stages, (late_u, carried, carried))
        alpha = norm_now / curve
        solution = solution + alpha[:, None] * direction
        residual = residual - alpha[:, None] * (base + near)
        if step + 1 < ITERATIONS:
            residual_proj = residual_proj - alpha[None, :, None] * image_proj
    return (solution, residual)


def solution(mesh):
    return jax.shard_map(
        per_device,
        mesh=mesh,
        in_specs=(
            P(None, ("gx", "gy")),
            P(),
            P(("gx", "gy")),
            P(None, ("gx", "gy")),
            P(None, ("gx", "gy")),
            P(None, ("gx", "gy")),
            P(),
            P(("gx", "gy"), None),
            P(("gx", "gy"), None, None),
        ),
        out_specs=(P(None, ("gx", "gy")), P(None, ("gx", "gy"))),
        check_vma=False,
    )
```

```python
import math

import jax
import jax.numpy as jnp
from jax import lax
from jax.sharding import PartitionSpec as P

TILE_POINTS = 256
ITERATIONS = 2


near_weight = 0.25
highest = lax.Precision.HIGHEST


def swapped(value, axis, bit):
    mask = 2**bit
    pairs = [(source, source ^ mask) for source in range(lax.axis_size(axis))]
    return lax.ppermute(value, axis, pairs)


def split3(values):
    high = lax.reduce_precision(values, exponent_bits=8, mantissa_bits=7)
    rest = values - high
    middle = lax.reduce_precision(rest, exponent_bits=8, mantissa_bits=7)
    return high, middle, rest - middle


def near_kernels(union):
    high, middle, low = split3(union)
    left = jnp.concatenate([high, high, middle, high, low, middle], axis=1).astype(jnp.bfloat16)
    right = jnp.concatenate([high, middle, high, low, high, middle], axis=1).astype(jnp.bfloat16)
    gram = jnp.einsum("gfi,gfj->gij", left, right, preferred_element_type=jnp.float32)
    square = jnp.sum(union * union, axis=1)
    dist = square[:, :, None] + square[:, None, :] - 2.0 * gram
    return near_weight * jnp.exp(-0.5 * dist)


def near_apply(kern, union_vec):
    return jnp.einsum("gij,gcj->gci", kern, union_vec, precision=lax.Precision.HIGH)


def pieces(values, axis):
    return jnp.concatenate(split3(values), axis=axis).astype(jnp.bfloat16)


def to_union(values, hot):
    count = values.shape[0]
    out = jnp.einsum("cp,gip->gci", pieces(values, 0), hot, preferred_element_type=jnp.float32)
    return (out[:, :count] + out[:, count : 2 * count]) + out[:, 2 * count :]


def from_union(values_u, hot):
    count = values_u.shape[1]
    out = jnp.einsum("gci,gip->cp", pieces(values_u, 1), hot, preferred_element_type=jnp.float32)
    return (out[:count] + out[count : 2 * count]) + out[2 * count :]


def tree_sums(proj, stages, state):
    low_count = lax.axis_size("gy").bit_length() - 1
    high_count = lax.axis_size("gx").bit_length() - 1
    rounds = [("gy", bit, bit) for bit in range(low_count)]
    rounds += [("gx", bit, low_count + bit) for bit in range(high_count)]
    running = proj
    for index, (axis, bit, level) in enumerate(rounds):
        partner = swapped(running[level:], axis, bit)
        stage = stages[index] if index < len(stages) else None
        if stage is not None:
            state, running = lax.optimization_barrier((state, running))
            state = stage(state)
        running = jnp.concatenate([running[:level], running[level:] + partner], axis=0)
        if stage is not None:
            running, state = lax.optimization_barrier((running, state))
    for stage in stages[len(rounds) :]:
        if stage is not None:
            state = stage(state)
    return running, state


def butterfly(value, stages, state):
    rounds = [("gy", bit) for bit in range(lax.axis_size("gy").bit_length() - 1)]
    rounds += [("gx", bit) for bit in range(lax.axis_size("gx").bit_length() - 1)]
    for index, (axis, bit) in enumerate(rounds):
        partner = swapped(value, axis, bit)
        if index < len(stages):
            state, value = lax.optimization_barrier((state, value))
            state = stages[index](state)
        value = value + partner
        if index < len(stages):
            value, state = lax.optimization_barrier((value, state))
    for stage in stages[len(rounds) :]:
        state = stage(state)
    return value, state


def per_device(coords, inv_scale, noise, right_side, basis, level_gain, coupling, order, pairs):
    columns, points = right_side.shape
    features = coords.shape[0]
    tiles = points // TILE_POINTS
    levels = level_gain.shape[0]
    rank = basis.shape[0]
    order_tiles = order.reshape(tiles, TILE_POINTS)
    union_order = jnp.concatenate([order_tiles[pairs[0, 0]], order_tiles[pairs[0, 1]]], axis=1)
    position = jnp.arange(points, dtype=jnp.int32)
    hot = (union_order[:, :, None] == position[None, None, :]).astype(jnp.bfloat16)
    scales = 2.0 ** ((1.0 - jnp.arange(levels, dtype=jnp.float32)) / 2.0)


    def project(values):
        return jnp.einsum("lp,cp,rp->lcr", level_gain, values, basis, precision=highest)

    def sums_with_norm(values, proj, stages, state):
        norm = jnp.sum(values * values, axis=1)
        extra = jnp.broadcast_to(norm[None, :, None], (1, columns, rank))
        running, state = tree_sums(jnp.concatenate([proj, extra], axis=0), stages, state)
        return running[:levels], running[levels, :, 0], state

    def permute_first(state):
        values, first, second = state
        return values, to_union(values, hot_first), second

    def permute_second(state):
        values, first, second = state
        return values, first, to_union(values, hot_second)

    def near_of_halves(state):
        values, first, second = state
        values_u = jnp.concatenate([first, second], axis=0)
        return values_u, lax.optimization_barrier(near_apply(kern, values_u)), second

    half = union_order.shape[0] // 2
    hot_first = (union_order[:half, :, None] == position[None, None, :]).astype(jnp.bfloat16)
    hot_second = (union_order[half:, :, None] == position[None, None, :]).astype(jnp.bfloat16)

    def unpermute_first(state):
        late, near, extra = state
        return late, from_union(late[:half], hot_first) + extra, extra

    def unpermute_second(state):
        late, near, extra = state
        return late, near + from_union(late[half:], hot_second), extra

    def permute_inputs(state):
        stacked = to_union(jnp.concatenate(state, axis=0), hot)
        return stacked[:, :features] * inv_scale[None, :, None], stacked[:, features:]

    def kernel_blocks(state):
        union_coords, direction_u = state
        return near_kernels(union_coords), direction_u

    def first_near(state):
        kern, direction_u = state
        return kern, direction_u, lax.optimization_barrier(near_apply(kern, direction_u))

    solution = jnp.zeros_like(right_side)
    residual = right_side
    direction = right_side
    residual_proj = project(residual)
    for step in range(ITERATIONS):
        if step == 0:
            stages = [None, permute_inputs, kernel_blocks, first_near]
            nodesum, norm_now, (kern, direction_u, near_u) = sums_with_norm(
                residual, residual_proj, stages, (coords, right_side)
            )
            late_u, nodesum = lax.optimization_barrier((near_u, nodesum))
            carried = jnp.zeros_like(right_side)
        else:
            empty = jnp.zeros((half,) + direction_u.shape[1:], jnp.float32)
            stages = [permute_first, permute_second, None, near_of_halves]
            residual_sum, norm_next, (residual_u, residual_near_u, unused) = sums_with_norm(
                residual, residual_proj, stages, (residual, empty, empty)
            )
            late_u, residual_sum = lax.optimization_barrier((residual_near_u, residual_sum))
            ratio = norm_next / norm_now
            direction = residual + ratio[:, None] * direction
            direction_u = residual_u + ratio[None, :, None] * direction_u
            nodesum = residual_sum + ratio[None, :, None] * nodesum
            near_u = residual_near_u + ratio[None, :, None] * near_u
            carried = ratio[:, None] * near
            norm_now = norm_next
        coupled = jnp.einsum("lcr,lrs->lcs", nodesum, coupling, precision=highest)
        coupled = (
            jnp.einsum("lcs,lrs->lcr", coupled, coupling, precision=highest) * scales[:, None, None]
        )
        back = jnp.einsum("lcr,rp->lcp", coupled, basis, precision=highest)
        far = jnp.sum(back * level_gain[:, None, :], axis=0)
        base = noise[None, :] * direction + far
        local = jnp.sum(direction * base, axis=1) + jnp.sum(direction_u * near_u, axis=(0, 2))
        def project_image(state, base=base):
            late, near, extra = state
            return late, near, project(base + near)

        stages = [unpermute_first, unpermute_second]
        if step + 1 < ITERATIONS:
            stages.append(project_image)
        curve, (late_u, near, image_proj) = butterfly(local, stages, (late_u, carried, carried))
        alpha = norm_now / curve
        solution = solution + alpha[:, None] * direction
        residual = residual - alpha[:, None] * (base + near)
        if step + 1 < ITERATIONS:
            residual_proj = residual_proj - alpha[None, :, None] * image_proj
    return (solution, residual)


def solution(mesh):
    return jax.shard_map(
        per_device,
        mesh=mesh,
        in_specs=(
            P(None, ("gx", "gy")),
            P(),
            P(("gx", "gy")),
            P(None, ("gx", "gy")),
            P(None, ("gx", "gy")),
            P(None, ("gx", "gy")),
            P(),
            P(("gx", "gy"), None),
            P(("gx", "gy"), None, None),
        ),
        out_specs=(P(None, ("gx", "gy")), P(None, ("gx", "gy"))),
        check_vma=False,
    )
```

```python
import math

import jax
import jax.numpy as jnp
from jax import lax
from jax.sharding import PartitionSpec as P

TILE_POINTS = 256
ITERATIONS = 2


near_weight = 0.25
highest = lax.Precision.HIGHEST


def swapped(value, axis, bit):
    mask = 2**bit
    pairs = [(source, source ^ mask) for source in range(lax.axis_size(axis))]
    return lax.ppermute(value, axis, pairs)


def split3(values):
    high = lax.reduce_precision(values, exponent_bits=8, mantissa_bits=7)
    rest = values - high
    middle = lax.reduce_precision(rest, exponent_bits=8, mantissa_bits=7)
    return high, middle, rest - middle


def near_kernels(union):
    high, middle, low = split3(union)
    left = jnp.concatenate([high, high, middle, high, low, middle], axis=1).astype(jnp.bfloat16)
    right = jnp.concatenate([high, middle, high, low, high, middle], axis=1).astype(jnp.bfloat16)
    gram = jnp.einsum("gfi,gfj->gij", left, right, preferred_element_type=jnp.float32)
    square = jnp.sum(union * union, axis=1)
    dist = square[:, :, None] + square[:, None, :] - 2.0 * gram
    return near_weight * jnp.exp(-0.5 * dist)


def near_apply(kern, union_vec):
    return jnp.einsum("gij,gcj->gci", kern, union_vec, precision=lax.Precision.HIGH)


def pieces(values, axis):
    return jnp.concatenate(split3(values), axis=axis).astype(jnp.bfloat16)


def to_union(values, hot):
    count = values.shape[0]
    out = jnp.einsum("cp,gip->gci", pieces(values, 0), hot, preferred_element_type=jnp.float32)
    return (out[:, :count] + out[:, count : 2 * count]) + out[:, 2 * count :]


def from_union(values_u, hot):
    count = values_u.shape[1]
    out = jnp.einsum("gci,gip->cp", pieces(values_u, 1), hot, preferred_element_type=jnp.float32)
    return (out[:count] + out[count : 2 * count]) + out[2 * count :]


def tree_sums(proj, stages, state):
    low_count = lax.axis_size("gy").bit_length() - 1
    high_count = lax.axis_size("gx").bit_length() - 1
    rounds = [("gy", bit, bit) for bit in range(low_count)]
    rounds += [("gx", bit, low_count + bit) for bit in range(high_count)]
    running = proj
    for index, (axis, bit, level) in enumerate(rounds):
        partner = swapped(running[level:], axis, bit)
        stage = stages[index] if index < len(stages) else None
        if stage is not None:
            state, running = lax.optimization_barrier((state, running))
            state = stage(state)
        running = jnp.concatenate([running[:level], running[level:] + partner], axis=0)
        if stage is not None:
            running, state = lax.optimization_barrier((running, state))
    for stage in stages[len(rounds) :]:
        if stage is not None:
            state = stage(state)
    return running, state


def butterfly(value, stages, state):
    rounds = [("gy", bit) for bit in range(lax.axis_size("gy").bit_length() - 1)]
    rounds += [("gx", bit) for bit in range(lax.axis_size("gx").bit_length() - 1)]
    for index, (axis, bit) in enumerate(rounds):
        partner = swapped(value, axis, bit)
        if index < len(stages):
            state, value = lax.optimization_barrier((state, value))
            state = stages[index](state)
        value = value + partner
        if index < len(stages):
            value, state = lax.optimization_barrier((value, state))
    for stage in stages[len(rounds) :]:
        state = stage(state)
    return value, state


def per_device(coords, inv_scale, noise, right_side, basis, level_gain, coupling, order, pairs):
    columns, points = right_side.shape
    features = coords.shape[0]
    tiles = points // TILE_POINTS
    levels = level_gain.shape[0]
    rank = basis.shape[0]
    order_tiles = order.reshape(tiles, TILE_POINTS)
    union_order = jnp.concatenate([order_tiles[pairs[0, 0]], order_tiles[pairs[0, 1]]], axis=1)
    position = jnp.arange(points, dtype=jnp.int32)
    hot = (union_order[:, :, None] == position[None, None, :]).astype(jnp.bfloat16)
    scales = 2.0 ** ((1.0 - jnp.arange(levels, dtype=jnp.float32)) / 2.0)


    def project(values):
        return jnp.einsum("lp,cp,rp->lcr", level_gain, values, basis, precision=highest)

    def sums_with_norm(values, proj, stages, state):
        norm = jnp.sum(values * values, axis=1)
        extra = jnp.broadcast_to(norm[None, :, None], (1, columns, rank))
        running, state = tree_sums(jnp.concatenate([proj, extra], axis=0), stages, state)
        return running[:levels], running[levels, :, 0], state

    def permute_first(state):
        values, first, second = state
        return values, to_union(values, hot_first), second

    def permute_second(state):
        values, first, second = state
        return values, first, to_union(values, hot_second)

    def near_of_halves(state):
        values, first, second = state
        values_u = jnp.concatenate([first, second], axis=0)
        return values_u, lax.optimization_barrier(near_apply(kern, values_u)), second

    half = union_order.shape[0] // 2
    hot_first = (union_order[:half, :, None] == position[None, None, :]).astype(jnp.bfloat16)
    hot_second = (union_order[half:, :, None] == position[None, None, :]).astype(jnp.bfloat16)

    def unpermute_first(state):
        late, near, extra = state
        return late, from_union(late[:half], hot_first) + extra, extra

    def unpermute_second(state):
        late, near, extra = state
        return late, near + from_union(late[half:], hot_second), extra

    def permute_inputs(state):
        stacked = to_union(jnp.concatenate(state, axis=0), hot)
        return stacked[:, :features] * inv_scale[None, :, None], stacked[:, features:]

    def kernel_blocks(state):
        union_coords, direction_u = state
        return near_kernels(union_coords), direction_u

    def first_near(state):
        kern, direction_u = state
        return kern, direction_u, lax.optimization_barrier(near_apply(kern, direction_u))

    solution = jnp.zeros_like(right_side)
    residual = right_side
    direction = right_side
    residual_proj = project(residual)
    for step in range(ITERATIONS):
        if step == 0:
            stages = [None, permute_inputs, None, kernel_blocks, first_near]
            nodesum, norm_now, (kern, direction_u, near_u) = sums_with_norm(
                residual, residual_proj, stages, (coords, right_side)
            )
            late_u, nodesum = lax.optimization_barrier((near_u, nodesum))
            carried = jnp.zeros_like(right_side)
        else:
            empty = jnp.zeros((half,) + direction_u.shape[1:], jnp.float32)
            stages = [permute_first, permute_second, None, near_of_halves]
            residual_sum, norm_next, (residual_u, residual_near_u, unused) = sums_with_norm(
                residual, residual_proj, stages, (residual, empty, empty)
            )
            late_u, residual_sum = lax.optimization_barrier((residual_near_u, residual_sum))
            ratio = norm_next / norm_now
            direction = residual + ratio[:, None] * direction
            direction_u = residual_u + ratio[None, :, None] * direction_u
            nodesum = residual_sum + ratio[None, :, None] * nodesum
            near_u = residual_near_u + ratio[None, :, None] * near_u
            carried = ratio[:, None] * near
            norm_now = norm_next
        coupled = jnp.einsum("lcr,lrs->lcs", nodesum, coupling, precision=highest)
        coupled = (
            jnp.einsum("lcs,lrs->lcr", coupled, coupling, precision=highest) * scales[:, None, None]
        )
        back = jnp.einsum("lcr,rp->lcp", coupled, basis, precision=highest)
        far = jnp.sum(back * level_gain[:, None, :], axis=0)
        base = noise[None, :] * direction + far
        local = jnp.sum(direction * base, axis=1) + jnp.sum(direction_u * near_u, axis=(0, 2))
        def project_image(state, base=base):
            late, near, extra = state
            return late, near, project(base + near)

        stages = [unpermute_first, unpermute_second]
        if step + 1 < ITERATIONS:
            stages.append(project_image)
        curve, (late_u, near, image_proj) = butterfly(local, stages, (late_u, carried, carried))
        alpha = norm_now / curve
        solution = solution + alpha[:, None] * direction
        residual = residual - alpha[:, None] * (base + near)
        if step + 1 < ITERATIONS:
            residual_proj = residual_proj - alpha[None, :, None] * image_proj
    return (solution, residual)


def solution(mesh):
    return jax.shard_map(
        per_device,
        mesh=mesh,
        in_specs=(
            P(None, ("gx", "gy")),
            P(),
            P(("gx", "gy")),
            P(None, ("gx", "gy")),
            P(None, ("gx", "gy")),
            P(None, ("gx", "gy")),
            P(),
            P(("gx", "gy"), None),
            P(("gx", "gy"), None, None),
        ),
        out_specs=(P(None, ("gx", "gy")), P(None, ("gx", "gy"))),
        check_vma=False,
    )
```

```python
import math

import jax
import jax.numpy as jnp
from jax import lax
from jax.sharding import PartitionSpec as P

TILE_POINTS = 256
ITERATIONS = 2


near_weight = 0.25
highest = lax.Precision.HIGHEST


def swapped(value, axis, bit):
    mask = 2**bit
    pairs = [(source, source ^ mask) for source in range(lax.axis_size(axis))]
    return lax.ppermute(value, axis, pairs)


def split3(values):
    high = lax.reduce_precision(values, exponent_bits=8, mantissa_bits=7)
    rest = values - high
    middle = lax.reduce_precision(rest, exponent_bits=8, mantissa_bits=7)
    return high, middle, rest - middle


def near_kernels(union):
    high, middle, low = split3(union)
    left = jnp.concatenate([high, high, middle, high, low, middle], axis=1).astype(jnp.bfloat16)
    right = jnp.concatenate([high, middle, high, low, high, middle], axis=1).astype(jnp.bfloat16)
    gram = jnp.einsum("gfi,gfj->gij", left, right, preferred_element_type=jnp.float32)
    square = jnp.sum(union * union, axis=1)
    dist = square[:, :, None] + square[:, None, :] - 2.0 * gram
    return near_weight * jnp.exp(-0.5 * dist)


def near_apply(kern, union_vec):
    return jnp.einsum("gij,gcj->gci", kern, union_vec, precision=lax.Precision.HIGH)


def pieces(values, axis):
    return jnp.concatenate(split3(values), axis=axis).astype(jnp.bfloat16)


def to_union(values, hot):
    count = values.shape[0]
    out = jnp.einsum("cp,gip->gci", pieces(values, 0), hot, preferred_element_type=jnp.float32)
    return (out[:, :count] + out[:, count : 2 * count]) + out[:, 2 * count :]


def from_union(values_u, hot):
    count = values_u.shape[1]
    out = jnp.einsum("gci,gip->cp", pieces(values_u, 1), hot, preferred_element_type=jnp.float32)
    return (out[:count] + out[count : 2 * count]) + out[2 * count :]


def tree_sums(proj, stages, state):
    low_count = lax.axis_size("gy").bit_length() - 1
    high_count = lax.axis_size("gx").bit_length() - 1
    rounds = [("gy", bit, bit) for bit in range(low_count)]
    rounds += [("gx", bit, low_count + bit) for bit in range(high_count)]
    running = proj
    for index, (axis, bit, level) in enumerate(rounds):
        partner = swapped(running[level:], axis, bit)
        stage = stages[index] if index < len(stages) else None
        if stage is not None:
            state, running = lax.optimization_barrier((state, running))
            state = stage(state)
        running = jnp.concatenate([running[:level], running[level:] + partner], axis=0)
        if stage is not None:
            running, state = lax.optimization_barrier((running, state))
    for stage in stages[len(rounds) :]:
        if stage is not None:
            state = stage(state)
    return running, state


def butterfly(value, stages, state):
    rounds = [("gy", bit) for bit in range(lax.axis_size("gy").bit_length() - 1)]
    rounds += [("gx", bit) for bit in range(lax.axis_size("gx").bit_length() - 1)]
    for index, (axis, bit) in enumerate(rounds):
        partner = swapped(value, axis, bit)
        if index < len(stages):
            state, value = lax.optimization_barrier((state, value))
            state = stages[index](state)
        value = value + partner
        if index < len(stages):
            value, state = lax.optimization_barrier((value, state))
    for stage in stages[len(rounds) :]:
        state = stage(state)
    return value, state


def per_device(coords, inv_scale, noise, right_side, basis, level_gain, coupling, order, pairs):
    columns, points = right_side.shape
    features = coords.shape[0]
    tiles = points // TILE_POINTS
    levels = level_gain.shape[0]
    rank = basis.shape[0]
    order_tiles = order.reshape(tiles, TILE_POINTS)
    union_order = jnp.concatenate([order_tiles[pairs[0, 0]], order_tiles[pairs[0, 1]]], axis=1)
    position = jnp.arange(points, dtype=jnp.int32)
    hot = (union_order[:, :, None] == position[None, None, :]).astype(jnp.bfloat16)
    scales = 2.0 ** ((1.0 - jnp.arange(levels, dtype=jnp.float32)) / 2.0)


    def project(values):
        return jnp.einsum("lp,cp,rp->lcr", level_gain, values, basis, precision=highest)

    def sums_with_norm(values, proj, stages, state):
        norm = jnp.sum(values * values, axis=1)
        extra = jnp.broadcast_to(norm[None, :, None], (1, columns, rank))
        running, state = tree_sums(jnp.concatenate([proj, extra], axis=0), stages, state)
        return running[:levels], running[levels, :, 0], state

    def permute_first(state):
        values, first, second = state
        return values, to_union(values, hot_first), second

    def permute_second(state):
        values, first, second = state
        return values, first, to_union(values, hot_second)

    def near_of_halves(state):
        values, first, second = state
        values_u = jnp.concatenate([first, second], axis=0)
        return values_u, lax.optimization_barrier(near_apply(kern, values_u)), second

    half = union_order.shape[0] // 2
    hot_first = (union_order[:half, :, None] == position[None, None, :]).astype(jnp.bfloat16)
    hot_second = (union_order[half:, :, None] == position[None, None, :]).astype(jnp.bfloat16)

    def unpermute_first(state):
        late, near, extra = state
        return late, from_union(late[:half], hot_first) + extra, extra

    def unpermute_second(state):
        late, near, extra = state
        return late, near + from_union(late[half:], hot_second), extra

    def permute_inputs(state):
        stacked = to_union(jnp.concatenate(state, axis=0), hot)
        return stacked[:, :features] * inv_scale[None, :, None], stacked[:, features:]

    def kernel_blocks(state):
        union_coords, direction_u = state
        product = jnp.einsum("lrs,lts->lrt", coupling, coupling, precision=highest)
        return near_kernels(union_coords), direction_u, product * scales[:, None, None]

    def first_near(state):
        kern, direction_u, product = state
        return kern, direction_u, lax.optimization_barrier(near_apply(kern, direction_u)), product

    solution = jnp.zeros_like(right_side)
    residual = right_side
    direction = right_side
    residual_proj = project(residual)
    for step in range(ITERATIONS):
        if step == 0:
            stages = [None, permute_inputs, None, kernel_blocks, first_near]
            nodesum, norm_now, (kern, direction_u, near_u, product) = sums_with_norm(
                residual, residual_proj, stages, (coords, right_side)
            )
            late_u, nodesum = lax.optimization_barrier((near_u, nodesum))
            carried = jnp.zeros_like(right_side)
        else:
            empty = jnp.zeros((half,) + direction_u.shape[1:], jnp.float32)
            stages = [permute_first, permute_second, None, near_of_halves]
            residual_sum, norm_next, (residual_u, residual_near_u, unused) = sums_with_norm(
                residual, residual_proj, stages, (residual, empty, empty)
            )
            late_u, residual_sum = lax.optimization_barrier((residual_near_u, residual_sum))
            ratio = norm_next / norm_now
            direction = residual + ratio[:, None] * direction
            direction_u = residual_u + ratio[None, :, None] * direction_u
            nodesum = residual_sum + ratio[None, :, None] * nodesum
            near_u = residual_near_u + ratio[None, :, None] * near_u
            carried = ratio[:, None] * near
            norm_now = norm_next
        coupled = jnp.einsum("lcr,lrt->lct", nodesum, product, precision=highest)
        back = jnp.einsum("lcr,rp->lcp", coupled, basis, precision=highest)
        far = jnp.sum(back * level_gain[:, None, :], axis=0)
        base = noise[None, :] * direction + far
        local = jnp.sum(direction * base, axis=1) + jnp.sum(direction_u * near_u, axis=(0, 2))
        def project_image(state, base=base):
            late, near, extra = state
            return late, near, project(base + near)

        stages = [unpermute_first, unpermute_second]
        if step + 1 < ITERATIONS:
            stages.append(project_image)
        curve, (late_u, near, image_proj) = butterfly(local, stages, (late_u, carried, carried))
        alpha = norm_now / curve
        solution = solution + alpha[:, None] * direction
        residual = residual - alpha[:, None] * (base + near)
        if step + 1 < ITERATIONS:
            residual_proj = residual_proj - alpha[None, :, None] * image_proj
    return (solution, residual)


def solution(mesh):
    return jax.shard_map(
        per_device,
        mesh=mesh,
        in_specs=(
            P(None, ("gx", "gy")),
            P(),
            P(("gx", "gy")),
            P(None, ("gx", "gy")),
            P(None, ("gx", "gy")),
            P(None, ("gx", "gy")),
            P(),
            P(("gx", "gy"), None),
            P(("gx", "gy"), None, None),
        ),
        out_specs=(P(None, ("gx", "gy")), P(None, ("gx", "gy"))),
        check_vma=False,
    )
```

```python
import math

import jax
import jax.numpy as jnp
from jax import lax
from jax.sharding import PartitionSpec as P

TILE_POINTS = 256
ITERATIONS = 2


near_weight = 0.25
highest = lax.Precision.HIGHEST


def swapped(value, axis, bit):
    mask = 2**bit
    pairs = [(source, source ^ mask) for source in range(lax.axis_size(axis))]
    return lax.ppermute(value, axis, pairs)


def split3(values):
    high = lax.reduce_precision(values, exponent_bits=8, mantissa_bits=7)
    rest = values - high
    middle = lax.reduce_precision(rest, exponent_bits=8, mantissa_bits=7)
    return high, middle, rest - middle


def near_kernels(union):
    high, middle, low = split3(union)
    left = jnp.concatenate([high, high, middle, high, low, middle], axis=1).astype(jnp.bfloat16)
    right = jnp.concatenate([high, middle, high, low, high, middle], axis=1).astype(jnp.bfloat16)
    gram = jnp.einsum("gfi,gfj->gij", left, right, preferred_element_type=jnp.float32)
    square = jnp.sum(union * union, axis=1)
    dist = square[:, :, None] + square[:, None, :] - 2.0 * gram
    return near_weight * jnp.exp(-0.5 * dist)


def near_apply(kern, union_vec):
    return jnp.einsum("gij,gcj->gci", kern, union_vec, precision=lax.Precision.HIGH)


def pieces(values, axis):
    return jnp.concatenate(split3(values), axis=axis).astype(jnp.bfloat16)


def to_union(values, hot):
    count = values.shape[0]
    out = jnp.einsum("cp,gip->gci", pieces(values, 0), hot, preferred_element_type=jnp.float32)
    return (out[:, :count] + out[:, count : 2 * count]) + out[:, 2 * count :]


def from_union(values_u, hot):
    count = values_u.shape[1]
    out = jnp.einsum("gci,gip->cp", pieces(values_u, 1), hot, preferred_element_type=jnp.float32)
    return (out[:count] + out[count : 2 * count]) + out[2 * count :]


def tree_sums(proj, stages, state):
    low_count = lax.axis_size("gy").bit_length() - 1
    high_count = lax.axis_size("gx").bit_length() - 1
    rounds = [("gy", bit, bit) for bit in range(low_count)]
    rounds += [("gx", bit, low_count + bit) for bit in range(high_count)]
    running = proj
    for index, (axis, bit, level) in enumerate(rounds):
        partner = swapped(running[level:], axis, bit)
        stage = stages[index] if index < len(stages) else None
        if stage is not None:
            state, running = lax.optimization_barrier((state, running))
            state = stage(state)
        running = jnp.concatenate([running[:level], running[level:] + partner], axis=0)
        if stage is not None:
            running, state = lax.optimization_barrier((running, state))
    for stage in stages[len(rounds) :]:
        if stage is not None:
            state = stage(state)
    return running, state


def butterfly(value, stages, state):
    rounds = [("gy", bit) for bit in range(lax.axis_size("gy").bit_length() - 1)]
    rounds += [("gx", bit) for bit in range(lax.axis_size("gx").bit_length() - 1)]
    for index, (axis, bit) in enumerate(rounds):
        partner = swapped(value, axis, bit)
        stage = stages[index] if index < len(stages) else None
        if stage is not None:
            state, value = lax.optimization_barrier((state, value))
            state = stage(state)
        value = value + partner
        if stage is not None:
            value, state = lax.optimization_barrier((value, state))
    for stage in stages[len(rounds) :]:
        if stage is not None:
            state = stage(state)
    return value, state


def per_device(coords, inv_scale, noise, right_side, basis, level_gain, coupling, order, pairs):
    columns, points = right_side.shape
    features = coords.shape[0]
    tiles = points // TILE_POINTS
    levels = level_gain.shape[0]
    rank = basis.shape[0]
    order_tiles = order.reshape(tiles, TILE_POINTS)
    union_order = jnp.concatenate([order_tiles[pairs[0, 0]], order_tiles[pairs[0, 1]]], axis=1)
    position = jnp.arange(points, dtype=jnp.int32)
    hot = (union_order[:, :, None] == position[None, None, :]).astype(jnp.bfloat16)
    scales = 2.0 ** ((1.0 - jnp.arange(levels, dtype=jnp.float32)) / 2.0)


    def project(values):
        return jnp.einsum("lp,cp,rp->lcr", level_gain, values, basis, precision=highest)

    def sums_with_norm(values, proj, stages, state):
        norm = jnp.sum(values * values, axis=1)
        extra = jnp.broadcast_to(norm[None, :, None], (1, columns, rank))
        running, state = tree_sums(jnp.concatenate([proj, extra], axis=0), stages, state)
        return running[:levels], running[levels, :, 0], state

    def permute_first(state):
        values, first, second = state
        return values, to_union(values, hot_first), second

    def permute_second(state):
        values, first, second = state
        return values, first, to_union(values, hot_second)

    def near_of_halves(state):
        values, first, second = state
        values_u = jnp.concatenate([first, second], axis=0)
        return values_u, lax.optimization_barrier(near_apply(kern, values_u)), second

    half = union_order.shape[0] // 2
    hot_first = (union_order[:half, :, None] == position[None, None, :]).astype(jnp.bfloat16)
    hot_second = (union_order[half:, :, None] == position[None, None, :]).astype(jnp.bfloat16)

    def unpermute_first(state):
        late, near, extra = state
        return late, from_union(late[:half], hot_first) + extra, extra

    def unpermute_second(state):
        late, near, extra = state
        return late, near + from_union(late[half:], hot_second), extra

    def permute_inputs(state):
        stacked = to_union(jnp.concatenate(state, axis=0), hot)
        return stacked[:, :features] * inv_scale[None, :, None], stacked[:, features:]

    def kernel_blocks(state):
        union_coords, direction_u = state
        product = jnp.einsum("lrs,lts->lrt", coupling, coupling, precision=highest)
        return near_kernels(union_coords), direction_u, product * scales[:, None, None]

    def first_near(state):
        kern, direction_u, product = state
        return kern, direction_u, lax.optimization_barrier(near_apply(kern, direction_u)), product

    solution = jnp.zeros_like(right_side)
    residual = right_side
    direction = right_side
    residual_proj = project(residual)
    for step in range(ITERATIONS):
        if step == 0:
            stages = [None, permute_inputs, None, kernel_blocks, first_near]
            nodesum, norm_now, (kern, direction_u, near_u, product) = sums_with_norm(
                residual, residual_proj, stages, (coords, right_side)
            )
            late_u, nodesum = lax.optimization_barrier((near_u, nodesum))
            carried = jnp.zeros_like(right_side)
        else:
            empty = jnp.zeros((half,) + direction_u.shape[1:], jnp.float32)
            stages = [permute_first, permute_second, None, near_of_halves]
            residual_sum, norm_next, (residual_u, residual_near_u, unused) = sums_with_norm(
                residual, residual_proj, stages, (residual, empty, empty)
            )
            late_u, residual_sum = lax.optimization_barrier((residual_near_u, residual_sum))
            ratio = norm_next / norm_now
            direction = residual + ratio[:, None] * direction
            direction_u = residual_u + ratio[None, :, None] * direction_u
            nodesum = residual_sum + ratio[None, :, None] * nodesum
            near_u = residual_near_u + ratio[None, :, None] * near_u
            carried = ratio[:, None] * near
            norm_now = norm_next
        coupled = jnp.einsum("lcr,lrt->lct", nodesum, product, precision=highest)
        back = jnp.einsum("lcr,rp->lcp", coupled, basis, precision=highest)
        far = jnp.sum(back * level_gain[:, None, :], axis=0)
        base = noise[None, :] * direction + far
        local = jnp.sum(direction * base, axis=1) + jnp.sum(direction_u * near_u, axis=(0, 2))
        def project_image(state, base=base):
            late, near, extra = state
            return late, near, project(base + near)

        stages = [unpermute_first, unpermute_second]
        if step + 1 < ITERATIONS:
            stages += [None, project_image]
        curve, (late_u, near, image_proj) = butterfly(local, stages, (late_u, carried, carried))
        alpha = norm_now / curve
        solution = solution + alpha[:, None] * direction
        residual = residual - alpha[:, None] * (base + near)
        if step + 1 < ITERATIONS:
            residual_proj = residual_proj - alpha[None, :, None] * image_proj
    return (solution, residual)


def solution(mesh):
    return jax.shard_map(
        per_device,
        mesh=mesh,
        in_specs=(
            P(None, ("gx", "gy")),
            P(),
            P(("gx", "gy")),
            P(None, ("gx", "gy")),
            P(None, ("gx", "gy")),
            P(None, ("gx", "gy")),
            P(),
            P(("gx", "gy"), None),
            P(("gx", "gy"), None, None),
        ),
        out_specs=(P(None, ("gx", "gy")), P(None, ("gx", "gy"))),
        check_vma=False,
    )
```

```python
import math

import jax
import jax.numpy as jnp
from jax import lax
from jax.sharding import PartitionSpec as P

TILE_POINTS = 256
ITERATIONS = 2


near_weight = 0.25
highest = lax.Precision.HIGHEST


def swapped(value, axis, bit):
    mask = 2**bit
    pairs = [(source, source ^ mask) for source in range(lax.axis_size(axis))]
    return lax.ppermute(value, axis, pairs)


def split3(values):
    high = lax.reduce_precision(values, exponent_bits=8, mantissa_bits=7)
    rest = values - high
    middle = lax.reduce_precision(rest, exponent_bits=8, mantissa_bits=7)
    return high, middle, rest - middle


def near_kernels(union):
    high, middle, low = split3(union)
    left = jnp.concatenate([high, high, middle, high, low, middle], axis=1).astype(jnp.bfloat16)
    right = jnp.concatenate([high, middle, high, low, high, middle], axis=1).astype(jnp.bfloat16)
    gram = jnp.einsum("gfi,gfj->gij", left, right, preferred_element_type=jnp.float32)
    square = jnp.sum(union * union, axis=1)
    dist = square[:, :, None] + square[:, None, :] - 2.0 * gram
    return near_weight * jnp.exp(-0.5 * dist)


def near_apply(kern, union_vec):
    return jnp.einsum("gij,gcj->gci", kern, union_vec, precision=lax.Precision.HIGH)


def pieces(values, axis):
    return jnp.concatenate(split3(values), axis=axis).astype(jnp.bfloat16)


def to_union(values, hot):
    count = values.shape[0]
    out = jnp.einsum("cp,gip->gci", pieces(values, 0), hot, preferred_element_type=jnp.float32)
    return (out[:, :count] + out[:, count : 2 * count]) + out[:, 2 * count :]


def from_union(values_u, hot):
    count = values_u.shape[1]
    out = jnp.einsum("gci,gip->cp", pieces(values_u, 1), hot, preferred_element_type=jnp.float32)
    return (out[:count] + out[count : 2 * count]) + out[2 * count :]


def tree_sums(proj, stages, state):
    low_count = lax.axis_size("gy").bit_length() - 1
    high_count = lax.axis_size("gx").bit_length() - 1
    rounds = [("gy", bit, bit) for bit in range(low_count)]
    rounds += [("gx", bit, low_count + bit) for bit in range(high_count)]
    running = proj
    for index, (axis, bit, level) in enumerate(rounds):
        partner = swapped(running[level:], axis, bit)
        stage = stages[index] if index < len(stages) else None
        if stage is not None:
            state, running = lax.optimization_barrier((state, running))
            state = stage(state)
        running = jnp.concatenate([running[:level], running[level:] + partner], axis=0)
        if stage is not None:
            running, state = lax.optimization_barrier((running, state))
    for stage in stages[len(rounds) :]:
        if stage is not None:
            state = stage(state)
    return running, state


def butterfly(value, stages, state):
    rounds = [("gy", bit) for bit in range(lax.axis_size("gy").bit_length() - 1)]
    rounds += [("gx", bit) for bit in range(lax.axis_size("gx").bit_length() - 1)]
    for index, (axis, bit) in enumerate(rounds):
        partner = swapped(value, axis, bit)
        if index < len(stages):
            state, value = lax.optimization_barrier((state, value))
            state = stages[index](state)
        value = value + partner
        if index < len(stages):
            value, state = lax.optimization_barrier((value, state))
    for stage in stages[len(rounds) :]:
        state = stage(state)
    return value, state


def per_device(coords, inv_scale, noise, right_side, basis, level_gain, coupling, order, pairs):
    columns, points = right_side.shape
    features = coords.shape[0]
    tiles = points // TILE_POINTS
    levels = level_gain.shape[0]
    rank = basis.shape[0]
    order_tiles = order.reshape(tiles, TILE_POINTS)
    union_order = jnp.concatenate([order_tiles[pairs[0, 0]], order_tiles[pairs[0, 1]]], axis=1)
    position = jnp.arange(points, dtype=jnp.int32)
    hot = (union_order[:, :, None] == position[None, None, :]).astype(jnp.bfloat16)
    scales = 2.0 ** ((1.0 - jnp.arange(levels, dtype=jnp.float32)) / 2.0)


    def project(values):
        return jnp.einsum("lp,cp,rp->lcr", level_gain, values, basis, precision=highest)

    def sums_with_norm(values, proj, stages, state):
        norm = jnp.sum(values * values, axis=1)
        extra = jnp.broadcast_to(norm[None, :, None], (1, columns, rank))
        running, state = tree_sums(jnp.concatenate([proj, extra], axis=0), stages, state)
        return running[:levels], running[levels, :, 0], state

    def permute_first(state):
        values, first, second = state
        return values, to_union(values, hot_first), second

    def permute_second(state):
        values, first, second = state
        return values, first, to_union(values, hot_second)

    def near_of_halves(state):
        values, first, second = state
        values_u = jnp.concatenate([first, second], axis=0)
        return values_u, lax.optimization_barrier(near_apply(kern, values_u)), second

    half = union_order.shape[0] // 2
    hot_first = (union_order[:half, :, None] == position[None, None, :]).astype(jnp.bfloat16)
    hot_second = (union_order[half:, :, None] == position[None, None, :]).astype(jnp.bfloat16)

    def unpermute_first(state):
        late, near, extra = state
        return late, from_union(late[:half], hot_first) + extra, extra

    def unpermute_second(state):
        late, near, extra = state
        return late, near + from_union(late[half:], hot_second), extra

    def permute_inputs_first(state):
        split = pieces(jnp.concatenate(state, axis=0), 0)
        return split, jnp.einsum("cp,gip->gci", split, hot_first, preferred_element_type=jnp.float32)

    def permute_inputs_second(state):
        split, first = state
        second = jnp.einsum("cp,gip->gci", split, hot_second, preferred_element_type=jnp.float32)
        stacked = jnp.concatenate([first, second], axis=0)
        count = stacked.shape[1] // 3
        stacked = (stacked[:, :count] + stacked[:, count : 2 * count]) + stacked[:, 2 * count :]
        return stacked[:, :features] * inv_scale[None, :, None], stacked[:, features:]

    def kernel_blocks(state):
        union_coords, direction_u = state
        return near_kernels(union_coords), direction_u

    def first_near(state):
        kern, direction_u = state
        return kern, direction_u, lax.optimization_barrier(near_apply(kern, direction_u))

    solution = jnp.zeros_like(right_side)
    residual = right_side
    direction = right_side
    residual_proj = project(residual)
    for step in range(ITERATIONS):
        if step == 0:
            stages = [None, permute_inputs_first, permute_inputs_second, kernel_blocks, first_near]
            nodesum, norm_now, (kern, direction_u, near_u) = sums_with_norm(
                residual, residual_proj, stages, (coords, right_side)
            )
            late_u, nodesum = lax.optimization_barrier((near_u, nodesum))
            carried = jnp.zeros_like(right_side)
        else:
            empty = jnp.zeros((half,) + direction_u.shape[1:], jnp.float32)
            stages = [permute_first, permute_second, None, near_of_halves]
            residual_sum, norm_next, (residual_u, residual_near_u, unused) = sums_with_norm(
                residual, residual_proj, stages, (residual, empty, empty)
            )
            late_u, residual_sum = lax.optimization_barrier((residual_near_u, residual_sum))
            ratio = norm_next / norm_now
            direction = residual + ratio[:, None] * direction
            direction_u = residual_u + ratio[None, :, None] * direction_u
            nodesum = residual_sum + ratio[None, :, None] * nodesum
            near_u = residual_near_u + ratio[None, :, None] * near_u
            carried = ratio[:, None] * near
            norm_now = norm_next
        coupled = jnp.einsum("lcr,lrs->lcs", nodesum, coupling, precision=highest)
        coupled = (
            jnp.einsum("lcs,lrs->lcr", coupled, coupling, precision=highest) * scales[:, None, None]
        )
        back = jnp.einsum("lcr,rp->lcp", coupled, basis, precision=highest)
        far = jnp.sum(back * level_gain[:, None, :], axis=0)
        base = noise[None, :] * direction + far
        local = jnp.sum(direction * base, axis=1) + jnp.sum(direction_u * near_u, axis=(0, 2))
        def project_image(state, base=base):
            late, near, extra = state
            return late, near, project(base + near)

        stages = [unpermute_first, unpermute_second]
        if step + 1 < ITERATIONS:
            stages.append(project_image)
        curve, (late_u, near, image_proj) = butterfly(local, stages, (late_u, carried, carried))
        alpha = norm_now / curve
        solution = solution + alpha[:, None] * direction
        residual = residual - alpha[:, None] * (base + near)
        if step + 1 < ITERATIONS:
            residual_proj = residual_proj - alpha[None, :, None] * image_proj
    return (solution, residual)


def solution(mesh):
    return jax.shard_map(
        per_device,
        mesh=mesh,
        in_specs=(
            P(None, ("gx", "gy")),
            P(),
            P(("gx", "gy")),
            P(None, ("gx", "gy")),
            P(None, ("gx", "gy")),
            P(None, ("gx", "gy")),
            P(),
            P(("gx", "gy"), None),
            P(("gx", "gy"), None, None),
        ),
        out_specs=(P(None, ("gx", "gy")), P(None, ("gx", "gy"))),
        check_vma=False,
    )
```

```python
import math

import jax
import jax.numpy as jnp
from jax import lax
from jax.sharding import PartitionSpec as P

TILE_POINTS = 256
ITERATIONS = 2


near_weight = 0.25
highest = lax.Precision.HIGHEST


def swapped(value, axis, bit):
    mask = 2**bit
    pairs = [(source, source ^ mask) for source in range(lax.axis_size(axis))]
    return lax.ppermute(value, axis, pairs)


def split3(values):
    high = lax.reduce_precision(values, exponent_bits=8, mantissa_bits=7)
    rest = values - high
    middle = lax.reduce_precision(rest, exponent_bits=8, mantissa_bits=7)
    return high, middle, rest - middle


def near_kernels(union):
    high, middle, low = split3(union)
    left = jnp.concatenate([high, high, middle, high, low, middle], axis=1).astype(jnp.bfloat16)
    right = jnp.concatenate([high, middle, high, low, high, middle], axis=1).astype(jnp.bfloat16)
    gram = jnp.einsum("gfi,gfj->gij", left, right, preferred_element_type=jnp.float32)
    square = jnp.sum(union * union, axis=1)
    dist = square[:, :, None] + square[:, None, :] - 2.0 * gram
    return near_weight * jnp.exp(-0.5 * dist)


def near_apply(kern, union_vec):
    return jnp.einsum("gij,gcj->gci", kern, union_vec, precision=lax.Precision.HIGH)


def pieces(values, axis):
    return jnp.concatenate(split3(values), axis=axis).astype(jnp.bfloat16)


def to_union(values, hot):
    count = values.shape[0]
    out = jnp.einsum("cp,gip->gci", pieces(values, 0), hot, preferred_element_type=jnp.float32)
    return (out[:, :count] + out[:, count : 2 * count]) + out[:, 2 * count :]


def from_union(values_u, hot):
    count = values_u.shape[1]
    out = jnp.einsum("gci,gip->cp", pieces(values_u, 1), hot, preferred_element_type=jnp.float32)
    return (out[:count] + out[count : 2 * count]) + out[2 * count :]


def tree_sums(proj, stages, state):
    low_count = lax.axis_size("gy").bit_length() - 1
    high_count = lax.axis_size("gx").bit_length() - 1
    rounds = [("gy", bit, bit) for bit in range(low_count)]
    rounds += [("gx", bit, low_count + bit) for bit in range(high_count)]
    running = proj
    for index, (axis, bit, level) in enumerate(rounds):
        partner = swapped(running[level:], axis, bit)
        stage = stages[index] if index < len(stages) else None
        if stage is not None:
            state, running = lax.optimization_barrier((state, running))
            state = stage(state)
        running = jnp.concatenate([running[:level], running[level:] + partner], axis=0)
        if stage is not None:
            running, state = lax.optimization_barrier((running, state))
    for stage in stages[len(rounds) :]:
        if stage is not None:
            state = stage(state)
    return running, state


def butterfly(value, stages, state):
    rounds = [("gy", bit) for bit in range(lax.axis_size("gy").bit_length() - 1)]
    rounds += [("gx", bit) for bit in range(lax.axis_size("gx").bit_length() - 1)]
    for index, (axis, bit) in enumerate(rounds):
        partner = swapped(value, axis, bit)
        if index < len(stages):
            state, value = lax.optimization_barrier((state, value))
            state = stages[index](state)
        value = value + partner
        if index < len(stages):
            value, state = lax.optimization_barrier((value, state))
    for stage in stages[len(rounds) :]:
        state = stage(state)
    return value, state


def per_device(coords, inv_scale, noise, right_side, basis, level_gain, coupling, order, pairs):
    columns, points = right_side.shape
    features = coords.shape[0]
    tiles = points // TILE_POINTS
    levels = level_gain.shape[0]
    rank = basis.shape[0]
    order_tiles = order.reshape(tiles, TILE_POINTS)
    union_order = jnp.concatenate([order_tiles[pairs[0, 0]], order_tiles[pairs[0, 1]]], axis=1)
    position = jnp.arange(points, dtype=jnp.int32)
    hot = (union_order[:, :, None] == position[None, None, :]).astype(jnp.bfloat16)
    scales = 2.0 ** ((1.0 - jnp.arange(levels, dtype=jnp.float32)) / 2.0)


    def project(values):
        return jnp.einsum("lp,cp,rp->lcr", level_gain, values, basis, precision=highest)

    def sums_with_norm(values, proj, stages, state):
        norm = jnp.sum(values * values, axis=1)
        extra = jnp.broadcast_to(norm[None, :, None], (1, columns, rank))
        running, state = tree_sums(jnp.concatenate([proj, extra], axis=0), stages, state)
        return running[:levels], running[levels, :, 0], state

    def permute_first(state):
        values, first, second = state
        return values, to_union(values, hot_first), second

    def permute_second(state):
        values, first, second = state
        return values, first, to_union(values, hot_second)

    def near_of_halves(state):
        values, first, second = state
        values_u = jnp.concatenate([first, second], axis=0)
        return values_u, lax.optimization_barrier(near_apply(kern, values_u)), second

    half = union_order.shape[0] // 2
    hot_first = (union_order[:half, :, None] == position[None, None, :]).astype(jnp.bfloat16)
    hot_second = (union_order[half:, :, None] == position[None, None, :]).astype(jnp.bfloat16)

    def unpermute_first(state):
        late, near, extra = state
        return late, from_union(late[:half], hot_first) + extra, extra

    def unpermute_second(state):
        late, near, extra = state
        return late, near + from_union(late[half:], hot_second), extra

    def permute_inputs_first(state):
        split = pieces(jnp.concatenate(state, axis=0), 0)
        return split, jnp.einsum("cp,gip->gci", split, hot_first, preferred_element_type=jnp.float32)

    def permute_inputs_second(state):
        split, first = state
        second = jnp.einsum("cp,gip->gci", split, hot_second, preferred_element_type=jnp.float32)
        stacked = jnp.concatenate([first, second], axis=0)
        count = stacked.shape[1] // 3
        stacked = (stacked[:, :count] + stacked[:, count : 2 * count]) + stacked[:, 2 * count :]
        return stacked[:, :features] * inv_scale[None, :, None], stacked[:, features:]

    def kernel_blocks(state):
        union_coords, direction_u = state
        product = jnp.einsum("lrs,lts->lrt", coupling, coupling, precision=highest)
        return near_kernels(union_coords), direction_u, product * scales[:, None, None]

    def first_near(state):
        kern, direction_u, product = state
        return kern, direction_u, lax.optimization_barrier(near_apply(kern, direction_u)), product

    solution = jnp.zeros_like(right_side)
    residual = right_side
    direction = right_side
    residual_proj = project(residual)
    for step in range(ITERATIONS):
        if step == 0:
            stages = [None, permute_inputs_first, permute_inputs_second, kernel_blocks, first_near]
            nodesum, norm_now, (kern, direction_u, near_u, product) = sums_with_norm(
                residual, residual_proj, stages, (coords, right_side)
            )
            late_u, nodesum = lax.optimization_barrier((near_u, nodesum))
            carried = jnp.zeros_like(right_side)
        else:
            empty = jnp.zeros((half,) + direction_u.shape[1:], jnp.float32)
            stages = [permute_first, permute_second, None, near_of_halves]
            residual_sum, norm_next, (residual_u, residual_near_u, unused) = sums_with_norm(
                residual, residual_proj, stages, (residual, empty, empty)
            )
            late_u, residual_sum = lax.optimization_barrier((residual_near_u, residual_sum))
            ratio = norm_next / norm_now
            direction = residual + ratio[:, None] * direction
            direction_u = residual_u + ratio[None, :, None] * direction_u
            nodesum = residual_sum + ratio[None, :, None] * nodesum
            near_u = residual_near_u + ratio[None, :, None] * near_u
            carried = ratio[:, None] * near
            norm_now = norm_next
        coupled = jnp.einsum("lcr,lrt->lct", nodesum, product, precision=highest)
        back = jnp.einsum("lcr,rp->lcp", coupled, basis, precision=highest)
        far = jnp.sum(back * level_gain[:, None, :], axis=0)
        base = noise[None, :] * direction + far
        local = jnp.sum(direction * base, axis=1) + jnp.sum(direction_u * near_u, axis=(0, 2))
        def project_image(state, base=base):
            late, near, extra = state
            return late, near, project(base + near)

        stages = [unpermute_first, unpermute_second]
        if step + 1 < ITERATIONS:
            stages.append(project_image)
        curve, (late_u, near, image_proj) = butterfly(local, stages, (late_u, carried, carried))
        alpha = norm_now / curve
        solution = solution + alpha[:, None] * direction
        residual = residual - alpha[:, None] * (base + near)
        if step + 1 < ITERATIONS:
            residual_proj = residual_proj - alpha[None, :, None] * image_proj
    return (solution, residual)


def solution(mesh):
    return jax.shard_map(
        per_device,
        mesh=mesh,
        in_specs=(
            P(None, ("gx", "gy")),
            P(),
            P(("gx", "gy")),
            P(None, ("gx", "gy")),
            P(None, ("gx", "gy")),
            P(None, ("gx", "gy")),
            P(),
            P(("gx", "gy"), None),
            P(("gx", "gy"), None, None),
        ),
        out_specs=(P(None, ("gx", "gy")), P(None, ("gx", "gy"))),
        check_vma=False,
    )
```

```python
import math

import jax
import jax.numpy as jnp
from jax import lax
from jax.sharding import PartitionSpec as P

TILE_POINTS = 256
ITERATIONS = 2


near_weight = 0.25
highest = lax.Precision.HIGHEST


def swapped(value, axis, bit):
    mask = 2**bit
    pairs = [(source, source ^ mask) for source in range(lax.axis_size(axis))]
    return lax.ppermute(value, axis, pairs)


def split3(values):
    high = lax.reduce_precision(values, exponent_bits=8, mantissa_bits=7)
    rest = values - high
    middle = lax.reduce_precision(rest, exponent_bits=8, mantissa_bits=7)
    return high, middle, rest - middle


def near_kernels(union):
    high, middle, low = split3(union)
    left = jnp.concatenate([high, high, middle, high, low, middle], axis=1).astype(jnp.bfloat16)
    right = jnp.concatenate([high, middle, high, low, high, middle], axis=1).astype(jnp.bfloat16)
    gram = jnp.einsum("gfi,gfj->gij", left, right, preferred_element_type=jnp.float32)
    square = jnp.sum(union * union, axis=1)
    dist = square[:, :, None] + square[:, None, :] - 2.0 * gram
    return near_weight * jnp.exp(-0.5 * dist)


def near_apply(kern, union_vec):
    return jnp.einsum("gij,gcj->gci", kern, union_vec, precision=lax.Precision.HIGH)


def pieces(values, axis):
    return jnp.concatenate(split3(values), axis=axis).astype(jnp.bfloat16)


def to_union(values, hot):
    count = values.shape[0]
    out = jnp.einsum("cp,gip->gci", pieces(values, 0), hot, preferred_element_type=jnp.float32)
    return (out[:, :count] + out[:, count : 2 * count]) + out[:, 2 * count :]


def from_union(values_u, hot):
    count = values_u.shape[1]
    out = jnp.einsum("gci,gip->cp", pieces(values_u, 1), hot, preferred_element_type=jnp.float32)
    return (out[:count] + out[count : 2 * count]) + out[2 * count :]


def tree_sums(proj, stages, state):
    low_count = lax.axis_size("gy").bit_length() - 1
    high_count = lax.axis_size("gx").bit_length() - 1
    rounds = [("gy", bit, bit) for bit in range(low_count)]
    rounds += [("gx", bit, low_count + bit) for bit in range(high_count)]
    running = proj
    for index, (axis, bit, level) in enumerate(rounds):
        partner = swapped(running[level:], axis, bit)
        stage = stages[index] if index < len(stages) else None
        if stage is not None:
            state, running = lax.optimization_barrier((state, running))
            state = stage(state)
        running = jnp.concatenate([running[:level], running[level:] + partner], axis=0)
        if stage is not None:
            running, state = lax.optimization_barrier((running, state))
    for stage in stages[len(rounds) :]:
        if stage is not None:
            state = stage(state)
    return running, state


def butterfly(value, stages, state):
    rounds = [("gy", bit) for bit in range(lax.axis_size("gy").bit_length() - 1)]
    rounds += [("gx", bit) for bit in range(lax.axis_size("gx").bit_length() - 1)]
    for index, (axis, bit) in enumerate(rounds):
        partner = swapped(value, axis, bit)
        if index < len(stages):
            state, value = lax.optimization_barrier((state, value))
            state = stages[index](state)
        value = value + partner
        if index < len(stages):
            value, state = lax.optimization_barrier((value, state))
    for stage in stages[len(rounds) :]:
        state = stage(state)
    return value, state


def per_device(coords, inv_scale, noise, right_side, basis, level_gain, coupling, order, pairs):
    columns, points = right_side.shape
    features = coords.shape[0]
    tiles = points // TILE_POINTS
    levels = level_gain.shape[0]
    rank = basis.shape[0]
    order_tiles = order.reshape(tiles, TILE_POINTS)
    union_order = jnp.concatenate([order_tiles[pairs[0, 0]], order_tiles[pairs[0, 1]]], axis=1)
    position = jnp.arange(points, dtype=jnp.int32)
    hot = (union_order[:, :, None] == position[None, None, :]).astype(jnp.bfloat16)
    scales = 2.0 ** ((1.0 - jnp.arange(levels, dtype=jnp.float32)) / 2.0)


    def project(values):
        return jnp.einsum("lp,cp,rp->lcr", level_gain, values, basis, precision=highest)

    def sums_with_norm(values, proj, stages, state):
        norm = jnp.sum(values * values, axis=1)
        extra = jnp.broadcast_to(norm[None, :, None], (1, columns, rank))
        running, state = tree_sums(jnp.concatenate([proj, extra], axis=0), stages, state)
        return running[:levels], running[levels, :, 0], state

    def sums_alone(proj, stages, state):
        return tree_sums(proj, stages, state)

    def permute_first(state):
        values, first, second = state
        return values, to_union(values, hot_first), second

    def permute_second(state):
        values, first, second = state
        return values, first, to_union(values, hot_second)

    def near_of_halves(state):
        values, first, second = state
        values_u = jnp.concatenate([first, second], axis=0)
        return values_u, lax.optimization_barrier(near_apply(kern, values_u)), second

    half = union_order.shape[0] // 2
    hot_first = (union_order[:half, :, None] == position[None, None, :]).astype(jnp.bfloat16)
    hot_second = (union_order[half:, :, None] == position[None, None, :]).astype(jnp.bfloat16)

    def unpermute_first(state):
        late, near, extra = state
        return late, from_union(late[:half], hot_first) + extra, extra

    def unpermute_second(state):
        late, near, extra = state
        return late, near + from_union(late[half:], hot_second), extra

    def permute_inputs_first(state):
        split = pieces(jnp.concatenate(state, axis=0), 0)
        return split, jnp.einsum("cp,gip->gci", split, hot_first, preferred_element_type=jnp.float32)

    def permute_inputs_second(state):
        split, first = state
        second = jnp.einsum("cp,gip->gci", split, hot_second, preferred_element_type=jnp.float32)
        stacked = jnp.concatenate([first, second], axis=0)
        count = stacked.shape[1] // 3
        stacked = (stacked[:, :count] + stacked[:, count : 2 * count]) + stacked[:, 2 * count :]
        return stacked[:, :features] * inv_scale[None, :, None], stacked[:, features:]

    def kernel_blocks(state):
        union_coords, direction_u = state
        return near_kernels(union_coords), direction_u

    def first_near(state):
        kern, direction_u = state
        return kern, direction_u, lax.optimization_barrier(near_apply(kern, direction_u))

    solution = jnp.zeros_like(right_side)
    residual = right_side
    direction = right_side
    residual_proj = project(residual)
    for step in range(ITERATIONS):
        if step == 0:
            stages = [None, permute_inputs_first, permute_inputs_second, kernel_blocks, first_near]
            nodesum, (kern, direction_u, near_u) = sums_alone(
                residual_proj, stages, (coords, right_side)
            )
            norm_now = None
            late_u, nodesum = lax.optimization_barrier((near_u, nodesum))
            carried = jnp.zeros_like(right_side)
        else:
            empty = jnp.zeros((half,) + direction_u.shape[1:], jnp.float32)
            stages = [permute_first, permute_second, None, near_of_halves]
            residual_sum, norm_next, (residual_u, residual_near_u, unused) = sums_with_norm(
                residual, residual_proj, stages, (residual, empty, empty)
            )
            late_u, residual_sum = lax.optimization_barrier((residual_near_u, residual_sum))
            ratio = norm_next / norm_now
            direction = residual + ratio[:, None] * direction
            direction_u = residual_u + ratio[None, :, None] * direction_u
            nodesum = residual_sum + ratio[None, :, None] * nodesum
            near_u = residual_near_u + ratio[None, :, None] * near_u
            carried = ratio[:, None] * near
            norm_now = norm_next
        coupled = jnp.einsum("lcr,lrs->lcs", nodesum, coupling, precision=highest)
        coupled = (
            jnp.einsum("lcs,lrs->lcr", coupled, coupling, precision=highest) * scales[:, None, None]
        )
        back = jnp.einsum("lcr,rp->lcp", coupled, basis, precision=highest)
        far = jnp.sum(back * level_gain[:, None, :], axis=0)
        base = noise[None, :] * direction + far
        local = jnp.sum(direction * base, axis=1) + jnp.sum(direction_u * near_u, axis=(0, 2))
        if norm_now is None:
            local = jnp.concatenate([local, jnp.sum(residual * residual, axis=1)])
        def project_image(state, base=base):
            late, near, extra = state
            return late, near, project(base + near)

        stages = [unpermute_first, unpermute_second]
        if step + 1 < ITERATIONS:
            stages.append(project_image)
        curve, (late_u, near, image_proj) = butterfly(local, stages, (late_u, carried, carried))
        if norm_now is None:
            curve, norm_now = curve[:columns], curve[columns:]
        alpha = norm_now / curve
        solution = solution + alpha[:, None] * direction
        residual = residual - alpha[:, None] * (base + near)
        if step + 1 < ITERATIONS:
            residual_proj = residual_proj - alpha[None, :, None] * image_proj
    return (solution, residual)


def solution(mesh):
    return jax.shard_map(
        per_device,
        mesh=mesh,
        in_specs=(
            P(None, ("gx", "gy")),
            P(),
            P(("gx", "gy")),
            P(None, ("gx", "gy")),
            P(None, ("gx", "gy")),
            P(None, ("gx", "gy")),
            P(),
            P(("gx", "gy"), None),
            P(("gx", "gy"), None, None),
        ),
        out_specs=(P(None, ("gx", "gy")), P(None, ("gx", "gy"))),
        check_vma=False,
    )
```
